32 devices in a mesh: groups: 2 (over x), tensor: 16 (over z, y, core).
Axes of the slice: x: 2, y: 2, z: 4, core: 2. Of those that a mesh axis runs over, the one named last changes fastest.
Arguments:
- tokens: bfloat16 [256, 8192], P(('groups', 'tensor')), parts along dimension 0, may hold values from -6 to 6
- gate_weight: bfloat16 [8192, 28672], P(None, 'tensor'), may hold values from -0.0625 to 0.0625
- up_weight: bfloat16 [8192, 28672], P(None, 'tensor'), may hold values from -0.0625 to 0.0625
- adapter_down_weight: bfloat16 [16, 8192, 64], P('tensor'), may hold values from -0.0625 to 0.0625
- adapter_up_weight: bfloat16 [16, 64, 28672], P(None, None, 'tensor'), may hold values from -0.75 to 0.75
- token_adapter_index: int32 [256, 1], P(('groups', 'tensor')), parts along dimension 0, may hold values from 0 to 15; in each aligned block of 128 rows (0 to 127, 128 to 255, ...) at most 16 rows name the same one
- adapter_slot_index: int32 [16], replicated, may hold values from 0 to 15, each once
Outputs:
- hidden: bfloat16 [256, 28672], P('groups', 'tensor'), parts along dimension 0
The draws below stay inside these ranges and needn't reach their ends.
There are 2 independent parts, one for each index of `groups`. The reference program is written for one: setup_inputs(seed, part) draws one part's arguments, and reference() takes and returns one part's arrays. A program takes and returns all parts, laid end to end along the dimension named above; an argument that names none is the same for every part. Nothing has to cross between parts.
Inputs may be any that keep to these rules, and one draw needn't show every extreme that they name: `token_adapter_index`: in every draw at most 16 of all 128 tokens use one adapter, and some adapter is used by exactly 16 tokens; every adapter is used by some token. `adapter_slot_index`: A permutation; slot s is stored on the device of index s along tensor.
All inputs are finite; a program needn't handle non-finite values.
Results may differ from the reference program's by a relative error of at most 0.0039.
Values may be sent and summed in bfloat16 or wider, within the bound.
No kernel may reach another device: no remote copies, remote signals or barrier semaphores. Data moves between devices by JAX's collectives and lax.ppermute only.
A program may use at most 192 MiB of HBM per device.

```python
import math
import jax
import jax.numpy as jnp
import numpy as np
from jax import lax

MODEL_WIDTH = 8192
HIDDEN_UNITS = 28672
ADAPTER_RANK = 64
TOKENS = 128
ADAPTER_COUNT = 16
CAP = 16


def levels(own_key, extent, cuts, low, top_value):
    def one(position, parts):
        heights = jax.random.uniform(jax.random.fold_in(jax.random.fold_in(own_key, 6), position), (parts,), jnp.float32, low / len(cuts), top_value / len(cuts))
        return jnp.repeat(jnp.exp(heights), extent[position] // parts).reshape((-1,) + (1,) * (len(extent) - position - 1))

    loudness = one(*cuts[0])
    for cut in cuts[1:]:
        loudness = loudness * one(*cut)
    return loudness


def deal_out(rng, own, number, rows, number_of, top, most, lean):
    ranking = jax.random.permutation(rng, number_of)
    heavy_load, usual = load_shares(number_of, rows * top, most, lean, True), load_shares(number_of, rows * top, most, lean, False)
    places = jnp.arange(number_of)

    def named(tallies, rotation):
        used = int((tallies > 0).sum())
        fixed = max(1, used // 4)
        shifted = fixed + (places - fixed + rotation * (used - fixed)) % max(1, number_of - fixed)
        return jnp.zeros((number_of,), jnp.int32).at[ranking[jnp.where(places < fixed, places, shifted)]].set(jnp.asarray(tallies, jnp.int32))

    tallies = jnp.where(number % 4 == 0, named(heavy_load, number // 4), named(usual, number - number // 4 - 1))
    mixed = jax.random.permutation(jax.random.fold_in(own, 3), number_of)
    source_of, sink = mixed[0:number_of // 2 * 2:2], mixed[1:number_of // 2 * 2:2]
    slack = jnp.minimum(tallies[source_of] - 1, most - tallies[sink]) // 2
    slack = jnp.where((source_of == ranking[0]) | (sink == ranking[0]) | (tallies[sink] == 0), 0, jnp.maximum(slack, 0))
    shifted = jax.random.randint(jax.random.fold_in(own, 4), (number_of // 2,), 0, 1 << 20) % (slack + 1)
    tallies = tallies.at[source_of].add(-shifted).at[sink].add(shifted)
    labels = jnp.searchsorted(jnp.cumsum(tallies), jnp.arange(rows * top), side="right").astype(jnp.int32)
    table = labels.reshape(top, rows).T
    table = table[jax.random.permutation(jax.random.fold_in(own, 1), rows)]
    rotation = jax.random.randint(jax.random.fold_in(own, 2), (rows, 1), 0, top)
    return jnp.take_along_axis(table, (jnp.arange(top)[None, :] + rotation) % top, axis=1)


def load_shares(number_of, total, bound, slope, full):
    loads = [(1 << 20) // math.isqrt(grade ** slope) + 1 for grade in range(1, number_of + 1)]
    largest = bound if full else min(bound, max(-(-total // number_of), total * loads[0] // sum(loads)))
    least = 1 if total - largest >= number_of - 1 else 0
    counts, spare = [largest] + [least] * (number_of - 1), total - largest - least * (number_of - 1)
    while spare > 0:
        free = [i for i in range(1, number_of) if counts[i] < largest] or [i for i in range(1, number_of) if counts[i] < bound]
        whole, left = sum([loads[i] for i in free]), spare
        for i in free:
            addition = min(bound - counts[i], max(1, left * loads[i] // whole), spare)
            counts[i] = counts[i] + addition
            spare = spare - addition
    return np.array(counts)


def centred(rng, extent, width, reach, shards=(), held_as=jnp.bfloat16):
    values = jax.random.normal(rng, extent, jnp.float32) * width
    if len(shards) > 0:
        values = levels(rng, extent, shards, -0.22, 0.18) * values
    return jnp.clip(values, min=-reach, max=reach).astype(held_as)


def setup_inputs(seed: int = 0, part: int = 0) -> dict:
    splits = jax.random.split(jax.random.key(seed), 8)
    part_keys = jax.random.split(jax.random.fold_in(splits[7], part), 8)
    tokens = centred(part_keys[0], (TOKENS, MODEL_WIDTH), 1.0, 6.0, ((0, 16),))
    gate_weight = centred(splits[1], (MODEL_WIDTH, HIDDEN_UNITS), MODEL_WIDTH ** -0.5, 0.0625, ((1, 16),))
    up_weight = centred(splits[2], (MODEL_WIDTH, HIDDEN_UNITS), MODEL_WIDTH ** -0.5, 0.0625, ((1, 16),))
    adapter_down_weight = centred(splits[3], (ADAPTER_COUNT, MODEL_WIDTH, ADAPTER_RANK), MODEL_WIDTH ** -0.5, 0.0625, ((0, 16),))
    adapter_up_weight = centred(splits[4], (ADAPTER_COUNT, ADAPTER_RANK, HIDDEN_UNITS), ADAPTER_RANK ** -0.5, 0.75, ((2, 16),))
    token_adapter_index_keys = jax.random.split(jax.random.fold_in(part_keys[5], 1), TOKENS // TOKENS)
    token_adapter_index_turns = jax.random.permutation(jax.random.fold_in(part_keys[5], 3), TOKENS // TOKENS)
    token_adapter_index = jax.vmap(lambda own, number: deal_out(jax.random.fold_in(part_keys[5], 2), own, number, TOKENS, ADAPTER_COUNT, 1, CAP, 2))(token_adapter_index_keys, token_adapter_index_turns).reshape((TOKENS, 1))
    adapter_slot_index = jax.random.permutation(splits[6], ADAPTER_COUNT).astype(jnp.int32)
    return {"tokens": tokens, "gate_weight": gate_weight, "up_weight": up_weight, "adapter_down_weight": adapter_down_weight, "adapter_up_weight": adapter_up_weight, "token_adapter_index": token_adapter_index, "adapter_slot_index": adapter_slot_index}


def reference(tokens, gate_weight, up_weight, adapter_down_weight, adapter_up_weight, token_adapter_index, adapter_slot_index):
    gate = jnp.dot(tokens, gate_weight, preferred_element_type=jnp.float32)
    up = jnp.dot(tokens, up_weight, preferred_element_type=jnp.float32)
    slots = adapter_slot_index[token_adapter_index[:, 0]].astype(jnp.int32)
    total = tokens.shape[0]
    rows_blocks = tokens.reshape(total // 16, 16, tokens.shape[1])
    slot_blocks = slots.reshape(total // 16, 16)

    def adapt(args):
        rows, selected_slot = args
        down_result = jnp.take(adapter_down_weight, selected_slot, axis=0).astype(jnp.float32)
        adapter_delta = jnp.einsum("td,tdr->tr", rows.astype(jnp.float32), down_result).astype(jnp.bfloat16)
        raised_output = jnp.take(adapter_up_weight, selected_slot, axis=0).astype(jnp.float32)
        return jnp.einsum("yl,ylh->yh", adapter_delta.astype(jnp.float32), raised_output)

    delta = lax.map(adapt, (rows_blocks, slot_blocks)).reshape(total, up_weight.shape[1])
    return (jax.nn.silu(gate) * (up + delta)).astype(jnp.bfloat16)
```

```python
import jax
import jax.numpy as jnp
from jax import lax
from jax.sharding import PartitionSpec as P

CHUNKS = 2
LANES = 128


def body(
    tokens,
    gate_weight,
    up_weight,
    adapter_down_weight,
    adapter_up_weight,
    token_adapter_index,
    adapter_slot_index,
):
    me = lax.axis_index("tensor")
    rows, width = tokens.shape
    step = width // CHUNKS
    local_slot = jnp.take(adapter_slot_index, token_adapter_index[:, 0], axis=0)
    slot_cols = jnp.broadcast_to(local_slot.astype(jnp.bfloat16)[:, None], (rows, LANES))

    gate = up = low = None
    slots = None
    for c in range(CHUNKS):
        piece = tokens[:, c * step : (c + 1) * step]
        if c == CHUNKS - 1:
            piece = jnp.concatenate([piece, slot_cols], axis=1)
        gathered = lax.all_gather(piece, "tensor", axis=0, tiled=True)
        if c == CHUNKS - 1:
            slots = gathered[:, step].astype(jnp.int32)
            gathered = gathered[:, :step]
        g = jnp.dot(gathered, gate_weight[c * step : (c + 1) * step], preferred_element_type=jnp.float32)
        u = jnp.dot(gathered, up_weight[c * step : (c + 1) * step], preferred_element_type=jnp.float32)
        d = jnp.dot(gathered, adapter_down_weight[0, c * step : (c + 1) * step], preferred_element_type=jnp.float32)
        gate = g if gate is None else gate + g
        up = u if up is None else up + u
        low = d if low is None else low + d

    mine = slots == me
    low = jnp.where(mine[:, None], low, 0.0).astype(jnp.bfloat16)
    spread = lax.all_gather(low, "tensor", axis=0, tiled=False)
    delta = jnp.einsum("str,srh->th", spread, adapter_up_weight, preferred_element_type=jnp.float32)
    return (jax.nn.silu(gate) * (up + delta)).astype(jnp.bfloat16)


def solution(mesh):
    in_specs = (
        P(("groups", "tensor"), None),
        P(None, "tensor"),
        P(None, "tensor"),
        P("tensor", None, None),
        P(None, None, "tensor"),
        P(("groups", "tensor"), None),
        P(),
    )
    out_specs = P("groups", "tensor")
    return jax.shard_map(body, mesh=mesh, in_specs=in_specs, out_specs=out_specs, check_vma=False)
```

```python
import jax
import jax.numpy as jnp
from jax import lax
from jax.sharding import PartitionSpec as P

LANES = 128
ASYNC_BYTES = 65536


def body(
    tokens,
    gate_weight,
    up_weight,
    adapter_down_weight,
    adapter_up_weight,
    token_adapter_index,
    adapter_slot_index,
):
    me = lax.axis_index("tensor")
    rows, width = tokens.shape
    local_slot = jnp.take(adapter_slot_index, token_adapter_index[:, 0], axis=0)
    slot_cols = jnp.broadcast_to(local_slot.astype(jnp.bfloat16)[:, None], (rows, LANES))
    gathered = lax.all_gather(jnp.concatenate([tokens, slot_cols], axis=1), "tensor", axis=0, tiled=True)
    slots = gathered[:, width].astype(jnp.int32)
    acts = gathered[:, :width]

    low = jnp.dot(acts, adapter_down_weight[0], preferred_element_type=jnp.float32)
    low = jnp.where((slots == me)[:, None], low, 0.0).astype(jnp.bfloat16)
    total, rank = low.shape
    padded = max(rank, -(-ASYNC_BYTES // (2 * total * LANES)) * LANES)
    low = jnp.pad(low, ((0, 0), (0, padded - rank)))
    spread = lax.all_gather(low, "tensor", axis=0, tiled=False)[:, :, :rank]

    gate = jnp.dot(acts, gate_weight, preferred_element_type=jnp.float32)
    up = jnp.dot(acts, up_weight, preferred_element_type=jnp.float32)
    gate, up = lax.optimization_barrier((gate, up))
    delta = jnp.einsum("str,srh->th", spread, adapter_up_weight, preferred_element_type=jnp.float32)
    return (jax.nn.silu(gate) * (up + delta)).astype(jnp.bfloat16)


def solution(mesh):
    in_specs = (
        P(("groups", "tensor"), None),
        P(None, "tensor"),
        P(None, "tensor"),
        P("tensor", None, None),
        P(None, None, "tensor"),
        P(("groups", "tensor"), None),
        P(),
    )
    out_specs = P("groups", "tensor")
    return jax.shard_map(body, mesh=mesh, in_specs=in_specs, out_specs=out_specs, check_vma=False)
```

```python
import jax
import jax.numpy as jnp
from jax import lax
from jax.sharding import PartitionSpec as P

LANES = 128
ASYNC_BYTES = 65536


def body(
    tokens,
    gate_weight,
    up_weight,
    adapter_down_weight,
    adapter_up_weight,
    token_adapter_index,
    adapter_slot_index,
):
    rows, width = tokens.shape
    acts = lax.all_gather(tokens, "tensor", axis=0, tiled=True)
    total = acts.shape[0]
    slots_held = adapter_up_weight.shape[0]

    low = jnp.dot(acts, adapter_down_weight[0], preferred_element_type=jnp.float32).astype(jnp.bfloat16)
    rank = low.shape[1]
    local_slot = jnp.take(adapter_slot_index, token_adapter_index[:, 0], axis=0).astype(jnp.bfloat16)
    padded = max(rank + LANES, -(-ASYNC_BYTES // (2 * total * LANES)) * LANES)
    slot_col = jnp.zeros((total,), jnp.bfloat16).at[:rows].set(local_slot)
    payload = jnp.concatenate(
        [low, slot_col[:, None], jnp.zeros((total, padded - rank - 1), jnp.bfloat16)], axis=1
    )
    gathered = lax.all_gather(payload, "tensor", axis=0, tiled=False)
    slots = gathered[:, :rows, rank].reshape(total).astype(jnp.int32)
    hits = slots[None, :, None] == jnp.arange(slots_held, dtype=jnp.int32)[:, None, None]
    spread = jnp.where(hits, gathered[:, :, :rank], jnp.zeros((), jnp.bfloat16))

    gate = jnp.dot(acts, gate_weight, preferred_element_type=jnp.float32)
    up = jnp.dot(acts, up_weight, preferred_element_type=jnp.float32)
    gate, up = lax.optimization_barrier((gate, up))
    delta = jnp.einsum("str,srh->th", spread, adapter_up_weight, preferred_element_type=jnp.float32)
    return (jax.nn.silu(gate) * (up + delta)).astype(jnp.bfloat16)


def solution(mesh):
    in_specs = (
        P(("groups", "tensor"), None),
        P(None, "tensor"),
        P(None, "tensor"),
        P("tensor", None, None),
        P(None, None, "tensor"),
        P(("groups", "tensor"), None),
        P(),
    )
    out_specs = P("groups", "tensor")
    return jax.shard_map(body, mesh=mesh, in_specs=in_specs, out_specs=out_specs, check_vma=False)
```

```python
import jax
import jax.numpy as jnp
from jax import lax
from jax.sharding import PartitionSpec as P

LANES = 128


def body(
    tokens,
    gate_weight,
    up_weight,
    adapter_down_weight,
    adapter_up_weight,
    token_adapter_index,
    adapter_slot_index,
):
    rows, width = tokens.shape
    acts = lax.all_gather(tokens, "tensor", axis=0, tiled=True)
    total = acts.shape[0]
    slots_held = adapter_up_weight.shape[0]

    low = jnp.dot(acts, adapter_down_weight[0], preferred_element_type=jnp.float32).astype(jnp.bfloat16)
    rank = low.shape[1]
    local_slot = jnp.take(adapter_slot_index, token_adapter_index[:, 0], axis=0).astype(jnp.bfloat16)
    padded = -(-(rank + 1) // LANES) * LANES
    slot_col = jnp.zeros((total,), jnp.bfloat16).at[:rows].set(local_slot)
    payload = jnp.concatenate(
        [low, slot_col[:, None], jnp.zeros((total, padded - rank - 1), jnp.bfloat16)], axis=1
    )
    copies = jnp.broadcast_to(payload[None], (slots_held,) + payload.shape)
    gathered = lax.all_to_all(copies, "tensor", 0, 0, tiled=False)
    slots = gathered[:, :rows, rank].reshape(total).astype(jnp.int32)
    hits = slots[None, :, None] == jnp.arange(slots_held, dtype=jnp.int32)[:, None, None]
    spread = jnp.where(hits, gathered[:, :, :rank], jnp.zeros((), jnp.bfloat16))

    gate = jnp.dot(acts, gate_weight, preferred_element_type=jnp.float32)
    up = jnp.dot(acts, up_weight, preferred_element_type=jnp.float32)
    gate, up = lax.optimization_barrier((gate, up))
    delta = jnp.einsum("str,srh->th", spread, adapter_up_weight, preferred_element_type=jnp.float32)
    return (jax.nn.silu(gate) * (up + delta)).astype(jnp.bfloat16)


def solution(mesh):
    in_specs = (
        P(("groups", "tensor"), None),
        P(None, "tensor"),
        P(None, "tensor"),
        P("tensor", None, None),
        P(None, None, "tensor"),
        P(("groups", "tensor"), None),
        P(),
    )
    out_specs = P("groups", "tensor")
    return jax.shard_map(body, mesh=mesh, in_specs=in_specs, out_specs=out_specs, check_vma=False)
```

```python
import jax
import jax.numpy as jnp
from jax import lax
from jax.experimental import pallas as pl
from jax.experimental.pallas import tpu as pltpu
from jax.sharding import PartitionSpec as P

LANES = 128
BLOCK_ROWS = 1024


def _projection_kernel(x_ref, gate_w_ref, up_w_ref, gate_ref, up_ref):
    @pl.when(pl.program_id(0) == 0)
    def _():
        gate_ref[...] = jnp.zeros_like(gate_ref)
        up_ref[...] = jnp.zeros_like(up_ref)

    x = x_ref[...]
    gate_ref[...] += jnp.dot(x, gate_w_ref[...], preferred_element_type=jnp.float32)
    up_ref[...] += jnp.dot(x, up_w_ref[...], preferred_element_type=jnp.float32)


def projections(acts, gate_weight, up_weight):
    total, width = acts.shape
    hidden = gate_weight.shape[1]
    step = min(BLOCK_ROWS, width)
    weight_bytes = 2 * width * hidden * gate_weight.dtype.itemsize
    return pl.pallas_call(
        _projection_kernel,
        grid=(width // step,),
        in_specs=[
            pl.BlockSpec((total, step), lambda k: (0, k)),
            pl.BlockSpec((step, hidden), lambda k: (k, 0)),
            pl.BlockSpec((step, hidden), lambda k: (k, 0)),
        ],
        out_specs=[
            pl.BlockSpec((total, hidden), lambda k: (0, 0)),
            pl.BlockSpec((total, hidden), lambda k: (0, 0)),
        ],
        out_shape=[jax.ShapeDtypeStruct((total, hidden), jnp.float32)] * 2,
        compiler_params=pltpu.CompilerParams(dimension_semantics=("arbitrary",)),
        cost_estimate=pl.CostEstimate(
            flops=4 * total * width * hidden,
            transcendentals=0,
            bytes_accessed=weight_bytes + total * width * 2 + 2 * total * hidden * 4,
        ),
    )(acts, gate_weight, up_weight)


def body(
    tokens,
    gate_weight,
    up_weight,
    adapter_down_weight,
    adapter_up_weight,
    token_adapter_index,
    adapter_slot_index,
):
    rows, width = tokens.shape
    acts = lax.all_gather(tokens, "tensor", axis=0, tiled=True)
    total = acts.shape[0]
    slots_held = adapter_up_weight.shape[0]

    low = jnp.dot(acts, adapter_down_weight[0], preferred_element_type=jnp.float32).astype(jnp.bfloat16)
    rank = low.shape[1]
    local_slot = jnp.take(adapter_slot_index, token_adapter_index[:, 0], axis=0).astype(jnp.bfloat16)
    padded = -(-(rank + 1) // LANES) * LANES
    slot_col = jnp.zeros((total,), jnp.bfloat16).at[:rows].set(local_slot)
    payload = jnp.concatenate(
        [low, slot_col[:, None], jnp.zeros((total, padded - rank - 1), jnp.bfloat16)], axis=1
    )
    copies = jnp.broadcast_to(payload[None], (slots_held,) + payload.shape)
    gathered = lax.all_to_all(copies, "tensor", 0, 0, tiled=False)
    slots = gathered[:, :rows, rank].reshape(total).astype(jnp.int32)
    hits = slots[None, :, None] == jnp.arange(slots_held, dtype=jnp.int32)[:, None, None]
    spread = jnp.where(hits, gathered[:, :, :rank], jnp.zeros((), jnp.bfloat16))

    gate, up = projections(acts, gate_weight, up_weight)
    delta = jnp.einsum("str,srh->th", spread, adapter_up_weight, preferred_element_type=jnp.float32)
    return (jax.nn.silu(gate) * (up + delta)).astype(jnp.bfloat16)


def solution(mesh):
    in_specs = (
        P(("groups", "tensor"), None),
        P(None, "tensor"),
        P(None, "tensor"),
        P("tensor", None, None),
        P(None, None, "tensor"),
        P(("groups", "tensor"), None),
        P(),
    )
    out_specs = P("groups", "tensor")
    return jax.shard_map(body, mesh=mesh, in_specs=in_specs, out_specs=out_specs, check_vma=False)
```

```python
import jax
import jax.numpy as jnp
from jax import lax
from jax.experimental import pallas as pl
from jax.experimental.pallas import tpu as pltpu
from jax.sharding import PartitionSpec as P

LANES = 128
BLOCK_ROWS = 1024


def _projection_kernel(x_ref, gate_w_ref, up_w_ref, *refs):
    if len(refs) == 4:
        gate_in_ref, up_in_ref, gate_ref, up_ref = refs
    else:
        gate_in_ref = up_in_ref = None
        gate_ref, up_ref = refs

    @pl.when(pl.program_id(0) == 0)
    def _():
        if gate_in_ref is None:
            gate_ref[...] = jnp.zeros_like(gate_ref)
            up_ref[...] = jnp.zeros_like(up_ref)
        else:
            gate_ref[...] = gate_in_ref[...]
            up_ref[...] = up_in_ref[...]

    x = x_ref[...]
    gate_ref[...] += jnp.dot(x, gate_w_ref[...], preferred_element_type=jnp.float32)
    up_ref[...] += jnp.dot(x, up_w_ref[...], preferred_element_type=jnp.float32)


def projections(acts, gate_weight, up_weight, first_row, partial=None):
    total, width = acts.shape
    hidden = gate_weight.shape[1]
    step = min(BLOCK_ROWS, width)
    offset = first_row // step
    weight_bytes = 2 * width * hidden * gate_weight.dtype.itemsize
    extra_specs = [] if partial is None else [pl.BlockSpec((total, hidden), lambda k: (0, 0))] * 2
    extra_args = () if partial is None else tuple(partial)
    return pl.pallas_call(
        _projection_kernel,
        grid=(width // step,),
        in_specs=[
            pl.BlockSpec((total, step), lambda k: (0, k)),
            pl.BlockSpec((step, hidden), lambda k: (k + offset, 0)),
            pl.BlockSpec((step, hidden), lambda k: (k + offset, 0)),
        ]
        + extra_specs,
        out_specs=[
            pl.BlockSpec((total, hidden), lambda k: (0, 0)),
            pl.BlockSpec((total, hidden), lambda k: (0, 0)),
        ],
        out_shape=[jax.ShapeDtypeStruct((total, hidden), jnp.float32)] * 2,
        compiler_params=pltpu.CompilerParams(dimension_semantics=("arbitrary",)),
        cost_estimate=pl.CostEstimate(
            flops=4 * total * width * hidden,
            transcendentals=0,
            bytes_accessed=weight_bytes + total * width * 2 + 2 * total * hidden * 4,
        ),
    )(acts, gate_weight, up_weight, *extra_args)


def body(
    tokens,
    gate_weight,
    up_weight,
    adapter_down_weight,
    adapter_up_weight,
    token_adapter_index,
    adapter_slot_index,
):
    rows, width = tokens.shape
    slots_held = adapter_up_weight.shape[0]
    half = width // 2
    acts_a = lax.all_gather(tokens[:, :half], "tensor", axis=0, tiled=True)
    copies = jnp.broadcast_to(tokens[None, :, half:], (slots_held, rows, width - half))
    acts_b = lax.all_to_all(copies, "tensor", 0, 0, tiled=False).reshape(slots_held * rows, width - half)
    total = acts_a.shape[0]

    down = adapter_down_weight[0]
    low = jnp.dot(acts_a, down[:half], preferred_element_type=jnp.float32)
    low = low + jnp.dot(acts_b, down[half:], preferred_element_type=jnp.float32)
    low = low.astype(jnp.bfloat16)
    rank = low.shape[1]
    local_slot = jnp.take(adapter_slot_index, token_adapter_index[:, 0], axis=0).astype(jnp.bfloat16)
    padded = -(-(rank + 1) // LANES) * LANES
    slot_col = jnp.zeros((total,), jnp.bfloat16).at[:rows].set(local_slot)
    payload = jnp.concatenate(
        [low, slot_col[:, None], jnp.zeros((total, padded - rank - 1), jnp.bfloat16)], axis=1
    )
    copies = jnp.broadcast_to(payload[None], (slots_held,) + payload.shape)
    gathered = lax.all_to_all(copies, "tensor", 0, 0, tiled=False)
    slots = gathered[:, :rows, rank].reshape(total).astype(jnp.int32)
    hits = slots[None, :, None] == jnp.arange(slots_held, dtype=jnp.int32)[:, None, None]
    spread = jnp.where(hits, gathered[:, :, :rank], jnp.zeros((), jnp.bfloat16))

    partial = projections(acts_b, gate_weight, up_weight, half)
    gate, up = projections(acts_a, gate_weight, up_weight, 0, partial)
    delta = jnp.einsum("str,srh->th", spread, adapter_up_weight, preferred_element_type=jnp.float32)
    return (jax.nn.silu(gate) * (up + delta)).astype(jnp.bfloat16)


def solution(mesh):
    in_specs = (
        P(("groups", "tensor"), None),
        P(None, "tensor"),
        P(None, "tensor"),
        P("tensor", None, None),
        P(None, None, "tensor"),
        P(("groups", "tensor"), None),
        P(),
    )
    out_specs = P("groups", "tensor")
    return jax.shard_map(body, mesh=mesh, in_specs=in_specs, out_specs=out_specs, check_vma=False)
```

```python
import jax
import jax.numpy as jnp
from jax import lax
from jax.experimental import pallas as pl
from jax.experimental.pallas import tpu as pltpu
from jax.sharding import PartitionSpec as P

LANES = 128
BLOCK_ROWS = 1024


def _projection_kernel(x_ref, gate_w_ref, up_w_ref, gate_ref, up_ref):
    @pl.when(pl.program_id(0) == 0)
    def _():
        gate_ref[...] = jnp.zeros_like(gate_ref)
        up_ref[...] = jnp.zeros_like(up_ref)

    x = x_ref[...]
    gate_ref[...] += jnp.dot(x, gate_w_ref[...], preferred_element_type=jnp.float32)
    up_ref[...] += jnp.dot(x, up_w_ref[...], preferred_element_type=jnp.float32)


def projections(acts, gate_weight, up_weight):
    total, width = acts.shape
    hidden = gate_weight.shape[1]
    step = min(BLOCK_ROWS, width)
    weight_bytes = 2 * width * hidden * gate_weight.dtype.itemsize
    return pl.pallas_call(
        _projection_kernel,
        grid=(width // step,),
        in_specs=[
            pl.BlockSpec((total, step), lambda k: (0, k)),
            pl.BlockSpec((step, hidden), lambda k: (k, 0)),
            pl.BlockSpec((step, hidden), lambda k: (k, 0)),
        ],
        out_specs=[
            pl.BlockSpec((total, hidden), lambda k: (0, 0)),
            pl.BlockSpec((total, hidden), lambda k: (0, 0)),
        ],
        out_shape=[jax.ShapeDtypeStruct((total, hidden), jnp.float32)] * 2,
        compiler_params=pltpu.CompilerParams(dimension_semantics=("arbitrary",)),
        cost_estimate=pl.CostEstimate(
            flops=4 * total * width * hidden,
            transcendentals=0,
            bytes_accessed=weight_bytes + total * width * 2 + 2 * total * hidden * 4,
        ),
    )(acts, gate_weight, up_weight)


def body(
    tokens,
    gate_weight,
    up_weight,
    adapter_down_weight,
    adapter_up_weight,
    token_adapter_index,
    adapter_slot_index,
):
    rows, width = tokens.shape
    slots_held = adapter_up_weight.shape[0]
    copies = jnp.broadcast_to(tokens[None], (slots_held,) + tokens.shape)
    acts = lax.all_to_all(copies, "tensor", 0, 0, tiled=False).reshape(slots_held * rows, width)
    total = acts.shape[0]

    low = jnp.dot(acts, adapter_down_weight[0], preferred_element_type=jnp.float32).astype(jnp.bfloat16)
    rank = low.shape[1]
    local_slot = jnp.take(adapter_slot_index, token_adapter_index[:, 0], axis=0).astype(jnp.bfloat16)
    padded = -(-(rank + 1) // LANES) * LANES
    slot_col = jnp.zeros((total,), jnp.bfloat16).at[:rows].set(local_slot)
    payload = jnp.concatenate(
        [low, slot_col[:, None], jnp.zeros((total, padded - rank - 1), jnp.bfloat16)], axis=1
    )
    copies = jnp.broadcast_to(payload[None], (slots_held,) + payload.shape)
    gathered = lax.all_to_all(copies, "tensor", 0, 0, tiled=False)
    slots = gathered[:, :rows, rank].reshape(total).astype(jnp.int32)
    hits = slots[None, :, None] == jnp.arange(slots_held, dtype=jnp.int32)[:, None, None]
    spread = jnp.where(hits, gathered[:, :, :rank], jnp.zeros((), jnp.bfloat16))

    gate, up = projections(acts, gate_weight, up_weight)
    delta = jnp.einsum("str,srh->th", spread, adapter_up_weight, preferred_element_type=jnp.float32)
    return (jax.nn.silu(gate) * (up + delta)).astype(jnp.bfloat16)


def solution(mesh):
    in_specs = (
        P(("groups", "tensor"), None),
        P(None, "tensor"),
        P(None, "tensor"),
        P("tensor", None, None),
        P(None, None, "tensor"),
        P(("groups", "tensor"), None),
        P(),
    )
    out_specs = P("groups", "tensor")
    return jax.shard_map(body, mesh=mesh, in_specs=in_specs, out_specs=out_specs, check_vma=False)
```

```python
import jax
import jax.numpy as jnp
from jax import lax
from jax.experimental import pallas as pl
from jax.experimental.pallas import tpu as pltpu
from jax.sharding import PartitionSpec as P

LANES = 128
BLOCK_ROWS = 1024


def _projection_kernel(order_ref, mine_ref, other_ref, gate_w_ref, up_w_ref, gate_ref, up_ref):
    k = pl.program_id(0)
    blocks = pl.num_programs(0) // 2

    @pl.when(k == 0)
    def _():
        gate_ref[...] = jnp.zeros_like(gate_ref)
        up_ref[...] = jnp.zeros_like(up_ref)

    def accumulate(x_ref):
        x = x_ref[...]
        gate_ref[...] += jnp.dot(x, gate_w_ref[...], preferred_element_type=jnp.float32)
        up_ref[...] += jnp.dot(x, up_w_ref[...], preferred_element_type=jnp.float32)

    pl.when(k < blocks)(lambda: accumulate(mine_ref))
    pl.when(k >= blocks)(lambda: accumulate(other_ref))


def projections(order, mine, other, gate_weight, up_weight):
    total, half = mine.shape
    hidden = gate_weight.shape[1]
    step = min(BLOCK_ROWS, half)
    blocks = half // step

    def weight_block(k, order_ref):
        first = order_ref[0] * blocks
        second = (1 - order_ref[0]) * blocks
        return (jnp.where(k < blocks, first + k, second + k - blocks), 0)

    weight_bytes = 2 * 2 * half * hidden * gate_weight.dtype.itemsize
    return pl.pallas_call(
        _projection_kernel,
        grid_spec=pltpu.PrefetchScalarGridSpec(
            num_scalar_prefetch=1,
            grid=(2 * blocks,),
            in_specs=[
                pl.BlockSpec((total, step), lambda k, o: (0, jnp.minimum(k, blocks - 1))),
                pl.BlockSpec((total, step), lambda k, o: (0, jnp.maximum(k - blocks, 0))),
                pl.BlockSpec((step, hidden), weight_block),
                pl.BlockSpec((step, hidden), weight_block),
            ],
            out_specs=[
                pl.BlockSpec((total, hidden), lambda k, o: (0, 0)),
                pl.BlockSpec((total, hidden), lambda k, o: (0, 0)),
            ],
        ),
        out_shape=[jax.ShapeDtypeStruct((total, hidden), jnp.float32)] * 2,
        compiler_params=pltpu.CompilerParams(dimension_semantics=("arbitrary",)),
        cost_estimate=pl.CostEstimate(
            flops=4 * total * 2 * half * hidden,
            transcendentals=0,
            bytes_accessed=weight_bytes + total * 2 * half * 2 + 2 * total * hidden * 4,
        ),
    )(order, mine, other, gate_weight, up_weight)


def body(
    tokens,
    gate_weight,
    up_weight,
    adapter_down_weight,
    adapter_up_weight,
    token_adapter_index,
    adapter_slot_index,
):
    rows, width = tokens.shape
    slots_held = adapter_up_weight.shape[0]
    half = width // 2
    me = lax.axis_index("tensor")
    order = me % 2
    halves = jnp.stack([tokens[:, :half], tokens[:, half:]])
    copies = jnp.broadcast_to(halves[None], (slots_held // 2, 2, rows, half)).reshape(slots_held, rows, half)
    mine = lax.all_to_all(copies, "tensor", 0, 0, tiled=False).reshape(slots_held * rows, half)
    other = lax.ppermute(mine, "tensor", [(j, j ^ 1) for j in range(slots_held)])
    total = mine.shape[0]

    down = adapter_down_weight[0]
    low = jnp.dot(mine, lax.dynamic_slice_in_dim(down, order * half, half), preferred_element_type=jnp.float32)
    low = low + jnp.dot(other, lax.dynamic_slice_in_dim(down, (1 - order) * half, half), preferred_element_type=jnp.float32)
    low = low.astype(jnp.bfloat16)
    rank = low.shape[1]
    local_slot = jnp.take(adapter_slot_index, token_adapter_index[:, 0], axis=0).astype(jnp.bfloat16)
    padded = -(-(rank + 1) // LANES) * LANES
    slot_col = jnp.zeros((total,), jnp.bfloat16).at[:rows].set(local_slot)
    payload = jnp.concatenate(
        [low, slot_col[:, None], jnp.zeros((total, padded - rank - 1), jnp.bfloat16)], axis=1
    )
    sent = jnp.broadcast_to(payload[None], (slots_held,) + payload.shape)
    gathered = lax.all_to_all(sent, "tensor", 0, 0, tiled=False)
    slots = gathered[:, :rows, rank].reshape(total).astype(jnp.int32)
    hits = slots[None, :, None] == jnp.arange(slots_held, dtype=jnp.int32)[:, None, None]
    spread = jnp.where(hits, gathered[:, :, :rank], jnp.zeros((), jnp.bfloat16))

    gate, up = projections(order.reshape(1).astype(jnp.int32), mine, other, gate_weight, up_weight)
    delta = jnp.einsum("str,srh->th", spread, adapter_up_weight, preferred_element_type=jnp.float32)
    return (jax.nn.silu(gate) * (up + delta)).astype(jnp.bfloat16)


def solution(mesh):
    in_specs = (
        P(("groups", "tensor"), None),
        P(None, "tensor"),
        P(None, "tensor"),
        P("tensor", None, None),
        P(None, None, "tensor"),
        P(("groups", "tensor"), None),
        P(),
    )
    out_specs = P("groups", "tensor")
    return jax.shard_map(body, mesh=mesh, in_specs=in_specs, out_specs=out_specs, check_vma=False)
```

```python
import jax
import jax.numpy as jnp
from jax import lax
from jax.experimental import pallas as pl
from jax.experimental.pallas import tpu as pltpu
from jax.sharding import PartitionSpec as P

LANES = 128
BLOCK_ROWS = 1024


def _projection_kernel(
    order_ref, mine_ref, other_ref, gate_w_ref, up_w_ref, spread_ref, lift_ref, out_ref, gate_ref, up_ref
):
    k = pl.program_id(0)
    blocks = pl.num_programs(0) // 2

    @pl.when(k == 0)
    def _():
        gate_ref[...] = jnp.zeros_like(gate_ref)
        up_ref[...] = jnp.zeros_like(up_ref)

    def accumulate(x_ref):
        x = x_ref[...]
        gate_ref[...] += jnp.dot(x, gate_w_ref[...], preferred_element_type=jnp.float32)
        up_ref[...] += jnp.dot(x, up_w_ref[...], preferred_element_type=jnp.float32)

    pl.when(k < blocks)(lambda: accumulate(mine_ref))
    pl.when(k >= blocks)(lambda: accumulate(other_ref))

    @pl.when(k == 2 * blocks - 1)
    def _():
        delta = jnp.dot(spread_ref[...], lift_ref[...], preferred_element_type=jnp.float32)
        out_ref[...] = (jax.nn.silu(gate_ref[...]) * (up_ref[...] + delta)).astype(out_ref.dtype)


def gated_hidden(order, mine, other, gate_weight, up_weight, spread, lift):
    total, half = mine.shape
    hidden = gate_weight.shape[1]
    step = min(BLOCK_ROWS, half)
    blocks = half // step

    def weight_block(k, order_ref):
        first = order_ref[0] * blocks
        second = (1 - order_ref[0]) * blocks
        return (jnp.where(k < blocks, first + k, second + k - blocks), 0)

    weight_bytes = 2 * 2 * half * hidden * gate_weight.dtype.itemsize
    return pl.pallas_call(
        _projection_kernel,
        grid_spec=pltpu.PrefetchScalarGridSpec(
            num_scalar_prefetch=1,
            grid=(2 * blocks,),
            in_specs=[
                pl.BlockSpec((total, step), lambda k, o: (0, jnp.minimum(k, blocks - 1))),
                pl.BlockSpec((total, step), lambda k, o: (0, jnp.maximum(k - blocks, 0))),
                pl.BlockSpec((step, hidden), weight_block),
                pl.BlockSpec((step, hidden), weight_block),
                pl.BlockSpec(spread.shape, lambda k, o: (0, 0)),
                pl.BlockSpec(lift.shape, lambda k, o: (0, 0)),
            ],
            out_specs=pl.BlockSpec((total, hidden), lambda k, o: (0, 0)),
            scratch_shapes=[pltpu.VMEM((total, hidden), jnp.float32)] * 2,
        ),
        out_shape=jax.ShapeDtypeStruct((total, hidden), jnp.bfloat16),
        compiler_params=pltpu.CompilerParams(dimension_semantics=("arbitrary",)),
        cost_estimate=pl.CostEstimate(
            flops=4 * total * 2 * half * hidden,
            transcendentals=0,
            bytes_accessed=weight_bytes + total * 2 * half * 2 + lift.size * 2 + total * hidden * 2,
        ),
    )(order, mine, other, gate_weight, up_weight, spread, lift)


def body(
    tokens,
    gate_weight,
    up_weight,
    adapter_down_weight,
    adapter_up_weight,
    token_adapter_index,
    adapter_slot_index,
):
    rows, width = tokens.shape
    slots_held = adapter_up_weight.shape[0]
    half = width // 2
    me = lax.axis_index("tensor")
    order = me % 2
    halves = jnp.stack([tokens[:, :half], tokens[:, half:]])
    copies = jnp.broadcast_to(halves[None], (slots_held // 2, 2, rows, half)).reshape(slots_held, rows, half)
    mine = lax.all_to_all(copies, "tensor", 0, 0, tiled=False).reshape(slots_held * rows, half)
    other = lax.ppermute(mine, "tensor", [(j, j ^ 1) for j in range(slots_held)])
    total = mine.shape[0]

    down = adapter_down_weight[0]
    low = jnp.dot(mine, lax.dynamic_slice_in_dim(down, order * half, half), preferred_element_type=jnp.float32)
    low = low + jnp.dot(other, lax.dynamic_slice_in_dim(down, (1 - order) * half, half), preferred_element_type=jnp.float32)
    low = low.astype(jnp.bfloat16)
    rank = low.shape[1]
    local_slot = jnp.take(adapter_slot_index, token_adapter_index[:, 0], axis=0).astype(jnp.bfloat16)
    padded = -(-(rank + 1) // LANES) * LANES
    slot_col = jnp.zeros((total,), jnp.bfloat16).at[:rows].set(local_slot)
    payload = jnp.concatenate(
        [low, slot_col[:, None], jnp.zeros((total, padded - rank - 1), jnp.bfloat16)], axis=1
    )
    sent = jnp.broadcast_to(payload[None], (slots_held,) + payload.shape)
    gathered = lax.all_to_all(sent, "tensor", 0, 0, tiled=False)
    slots = gathered[:, :rows, rank].reshape(total).astype(jnp.int32)
    hits = slots[None, :, None] == jnp.arange(slots_held, dtype=jnp.int32)[:, None, None]
    spread = jnp.where(hits, gathered[:, :, :rank], jnp.zeros((), jnp.bfloat16))
    spread = spread.transpose(1, 0, 2).reshape(total, slots_held * rank)
    lift = adapter_up_weight.reshape(slots_held * rank, adapter_up_weight.shape[2])
    order = order.reshape(1).astype(jnp.int32)
    return gated_hidden(order, mine, other, gate_weight, up_weight, spread, lift)


def solution(mesh):
    in_specs = (
        P(("groups", "tensor"), None),
        P(None, "tensor"),
        P(None, "tensor"),
        P("tensor", None, None),
        P(None, None, "tensor"),
        P(("groups", "tensor"), None),
        P(),
    )
    out_specs = P("groups", "tensor")
    return jax.shard_map(body, mesh=mesh, in_specs=in_specs, out_specs=out_specs, check_vma=False)
```

```python
import jax
import jax.numpy as jnp
from jax import lax
from jax.experimental import pallas as pl
from jax.experimental.pallas import tpu as pltpu
from jax.sharding import PartitionSpec as P

LANES = 128
BLOCK_ROWS = 1024


def _projection_kernel(order_ref, mine_ref, other_ref, gate_w_ref, up_w_ref, gate_ref, up_ref):
    k = pl.program_id(0)
    blocks = pl.num_programs(0) // 2

    @pl.when(k == 0)
    def _():
        gate_ref[...] = jnp.zeros_like(gate_ref)
        up_ref[...] = jnp.zeros_like(up_ref)

    def accumulate(x_ref):
        x = x_ref[...]
        gate_ref[...] += jnp.dot(x, gate_w_ref[...], preferred_element_type=jnp.float32)
        up_ref[...] += jnp.dot(x, up_w_ref[...], preferred_element_type=jnp.float32)

    pl.when(k < blocks)(lambda: accumulate(mine_ref))
    pl.when(k >= blocks)(lambda: accumulate(other_ref))


def projections(order, mine, other, gate_weight, up_weight):
    total, half = mine.shape
    hidden = gate_weight.shape[1]
    step = min(BLOCK_ROWS, half)
    blocks = half // step

    def weight_block(k, order_ref):
        first = order_ref[0] * blocks
        second = (1 - order_ref[0]) * blocks
        return (jnp.where(k < blocks, first + k, second + k - blocks), 0)

    weight_bytes = 2 * 2 * half * hidden * gate_weight.dtype.itemsize
    return pl.pallas_call(
        _projection_kernel,
        grid_spec=pltpu.PrefetchScalarGridSpec(
            num_scalar_prefetch=1,
            grid=(2 * blocks,),
            in_specs=[
                pl.BlockSpec((total, step), lambda k, o: (0, jnp.minimum(k, blocks - 1))),
                pl.BlockSpec((total, step), lambda k, o: (0, jnp.maximum(k - blocks, 0))),
                pl.BlockSpec((step, hidden), weight_block),
                pl.BlockSpec((step, hidden), weight_block),
            ],
            out_specs=[
                pl.BlockSpec((total, hidden), lambda k, o: (0, 0)),
                pl.BlockSpec((total, hidden), lambda k, o: (0, 0)),
            ],
        ),
        out_shape=[jax.ShapeDtypeStruct((total, hidden), jnp.float32)] * 2,
        compiler_params=pltpu.CompilerParams(dimension_semantics=("arbitrary",)),
        cost_estimate=pl.CostEstimate(
            flops=4 * total * 2 * half * hidden,
            transcendentals=0,
            bytes_accessed=weight_bytes + total * 2 * half * 2 + 2 * total * hidden * 4,
        ),
    )(order, mine, other, gate_weight, up_weight)


def _gating_kernel(slot_ref, gathered_ref, lift_ref, gate_ref, up_ref, out_ref):
    slot = slot_ref[...]
    rank = lift_ref.shape[1]
    slots_held = lift_ref.shape[0]

    def add_slot(s, delta):
        rows = jnp.where(slot == s, gathered_ref[s][:, :rank], jnp.zeros((), gathered_ref.dtype))
        return delta + jnp.dot(rows, lift_ref[s], preferred_element_type=jnp.float32)

    delta = lax.fori_loop(0, slots_held, add_slot, jnp.zeros(out_ref.shape, jnp.float32), unroll=min(slots_held, 16))
    gate = gate_ref[...]
    out_ref[...] = (jax.nn.silu(gate) * (up_ref[...] + delta)).astype(out_ref.dtype)


def gated_hidden(slot, gathered, lift, gate, up):
    total, hidden = gate.shape
    slots_held, rank, _ = lift.shape
    cols = 256 if hidden % 256 == 0 else hidden
    return pl.pallas_call(
        _gating_kernel,
        grid=(hidden // cols,),
        in_specs=[
            pl.BlockSpec(slot.shape, lambda j: (0, 0)),
            pl.BlockSpec(gathered.shape, lambda j: (0, 0, 0)),
            pl.BlockSpec((slots_held, rank, cols), lambda j: (0, 0, j)),
            pl.BlockSpec((total, cols), lambda j: (0, j)),
            pl.BlockSpec((total, cols), lambda j: (0, j)),
        ],
        out_specs=pl.BlockSpec((total, cols), lambda j: (0, j)),
        out_shape=jax.ShapeDtypeStruct((total, hidden), jnp.bfloat16),
        compiler_params=pltpu.CompilerParams(dimension_semantics=("arbitrary",)),
        cost_estimate=pl.CostEstimate(
            flops=2 * total * slots_held * rank * hidden,
            transcendentals=total * hidden,
            bytes_accessed=lift.size * 2 + gathered.size * 2 + 2 * total * hidden * 4 + total * hidden * 2,
        ),
    )(slot, gathered, lift, gate, up)


def body(
    tokens,
    gate_weight,
    up_weight,
    adapter_down_weight,
    adapter_up_weight,
    token_adapter_index,
    adapter_slot_index,
):
    rows, width = tokens.shape
    slots_held = adapter_up_weight.shape[0]
    half = width // 2
    me = lax.axis_index("tensor")
    order = me % 2
    halves = jnp.stack([tokens[:, :half], tokens[:, half:]])
    copies = jnp.broadcast_to(halves[None], (slots_held // 2, 2, rows, half)).reshape(slots_held, rows, half)
    mine = lax.all_to_all(copies, "tensor", 0, 0, tiled=False).reshape(slots_held * rows, half)
    other = lax.ppermute(mine, "tensor", [(j, j ^ 1) for j in range(slots_held)])
    total = mine.shape[0]

    down = adapter_down_weight[0]
    low = jnp.dot(mine, lax.dynamic_slice_in_dim(down, order * half, half), preferred_element_type=jnp.float32)
    low = low + jnp.dot(other, lax.dynamic_slice_in_dim(down, (1 - order) * half, half), preferred_element_type=jnp.float32)
    low = low.astype(jnp.bfloat16)
    rank = low.shape[1]
    local_slot = jnp.take(adapter_slot_index, token_adapter_index[:, 0], axis=0).astype(jnp.bfloat16)
    padded = -(-(rank + 1) // LANES) * LANES
    slot_col = jnp.zeros((total,), jnp.bfloat16).at[:rows].set(local_slot)
    payload = jnp.concatenate(
        [low, slot_col[:, None], jnp.zeros((total, padded - rank - 1), jnp.bfloat16)], axis=1
    )
    sent = jnp.broadcast_to(payload[None], (slots_held,) + payload.shape)
    gathered = lax.all_to_all(sent, "tensor", 0, 0, tiled=False)
    slots = gathered[:, :rows, rank].reshape(total, 1).astype(jnp.int32)

    gate, up = projections(order.reshape(1).astype(jnp.int32), mine, other, gate_weight, up_weight)
    return gated_hidden(slots, gathered, adapter_up_weight, gate, up)


def solution(mesh):
    in_specs = (
        P(("groups", "tensor"), None),
        P(None, "tensor"),
        P(None, "tensor"),
        P("tensor", None, None),
        P(None, None, "tensor"),
        P(("groups", "tensor"), None),
        P(),
    )
    out_specs = P("groups", "tensor")
    return jax.shard_map(body, mesh=mesh, in_specs=in_specs, out_specs=out_specs, check_vma=False)
```

```python
import jax
import jax.numpy as jnp
from jax import lax
from jax.experimental import pallas as pl
from jax.experimental.pallas import tpu as pltpu
from jax.sharding import PartitionSpec as P

LANES = 128
BLOCK_ROWS = 1024
PIECES = 2


def _projection_kernel(base_ref, mine_ref, other_ref, gate_w_ref, up_w_ref, *refs):
    if len(refs) == 4:
        gate_in_ref, up_in_ref, gate_ref, up_ref = refs
    else:
        gate_in_ref = up_in_ref = None
        gate_ref, up_ref = refs
    k = pl.program_id(0)
    blocks = pl.num_programs(0) // 2

    @pl.when(k == 0)
    def _():
        if gate_in_ref is None:
            gate_ref[...] = jnp.zeros_like(gate_ref)
            up_ref[...] = jnp.zeros_like(up_ref)
        else:
            gate_ref[...] = gate_in_ref[...]
            up_ref[...] = up_in_ref[...]

    def accumulate(x_ref):
        x = x_ref[...]
        gate_ref[...] += jnp.dot(x, gate_w_ref[...], preferred_element_type=jnp.float32)
        up_ref[...] += jnp.dot(x, up_w_ref[...], preferred_element_type=jnp.float32)

    pl.when(k < blocks)(lambda: accumulate(mine_ref))
    pl.when(k >= blocks)(lambda: accumulate(other_ref))


def projections(base, mine, other, gate_weight, up_weight, partial=None):
    total, half = mine.shape
    hidden = gate_weight.shape[1]
    step = min(BLOCK_ROWS, half)
    blocks = half // step

    def weight_block(k, base_ref):
        return (jnp.where(k < blocks, base_ref[0] + k, base_ref[1] + k - blocks), 0)

    extra_specs = [] if partial is None else [pl.BlockSpec((total, hidden), lambda k, o: (0, 0))] * 2
    extra_args = () if partial is None else tuple(partial)
    weight_bytes = 2 * 2 * half * hidden * gate_weight.dtype.itemsize
    return pl.pallas_call(
        _projection_kernel,
        grid_spec=pltpu.PrefetchScalarGridSpec(
            num_scalar_prefetch=1,
            grid=(2 * blocks,),
            in_specs=[
                pl.BlockSpec((total, step), lambda k, o: (0, jnp.minimum(k, blocks - 1))),
                pl.BlockSpec((total, step), lambda k, o: (0, jnp.maximum(k - blocks, 0))),
                pl.BlockSpec((step, hidden), weight_block),
                pl.BlockSpec((step, hidden), weight_block),
            ]
            + extra_specs,
            out_specs=[
                pl.BlockSpec((total, hidden), lambda k, o: (0, 0)),
                pl.BlockSpec((total, hidden), lambda k, o: (0, 0)),
            ],
        ),
        out_shape=[jax.ShapeDtypeStruct((total, hidden), jnp.float32)] * 2,
        compiler_params=pltpu.CompilerParams(dimension_semantics=("arbitrary",)),
        cost_estimate=pl.CostEstimate(
            flops=4 * total * 2 * half * hidden,
            transcendentals=0,
            bytes_accessed=weight_bytes + total * 2 * half * 2 + 2 * total * hidden * 4,
        ),
    )(base, mine, other, gate_weight, up_weight, *extra_args)


def body(
    tokens,
    gate_weight,
    up_weight,
    adapter_down_weight,
    adapter_up_weight,
    token_adapter_index,
    adapter_slot_index,
):
    rows, width = tokens.shape
    slots_held = adapter_up_weight.shape[0]
    half = width // 2
    piece = half // PIECES
    step = min(BLOCK_ROWS, piece)
    me = lax.axis_index("tensor")
    order = me % 2
    down = adapter_down_weight[0]
    partial = None
    low = None
    for q in range(PIECES):
        cols = [tokens[:, h * half + q * piece : h * half + (q + 1) * piece] for h in range(2)]
        copies = jnp.broadcast_to(jnp.stack(cols)[None], (slots_held // 2, 2, rows, piece))
        mine = lax.all_to_all(copies.reshape(slots_held, rows, piece), "tensor", 0, 0, tiled=False)
        mine = mine.reshape(slots_held * rows, piece)
        if partial is not None:
            mine, partial = lax.optimization_barrier((mine, partial))
        other = lax.ppermute(mine, "tensor", [(j, j ^ 1) for j in range(slots_held)])
        first = order * half + q * piece
        second = (1 - order) * half + q * piece
        base = jnp.stack([first // step, second // step]).astype(jnp.int32)
        partial = projections(base, mine, other, gate_weight, up_weight, partial)
        part = jnp.dot(mine, lax.dynamic_slice_in_dim(down, first, piece), preferred_element_type=jnp.float32)
        part = part + jnp.dot(other, lax.dynamic_slice_in_dim(down, second, piece), preferred_element_type=jnp.float32)
        low = part if low is None else low + part
    total = mine.shape[0]
    gate, up = partial
    low = low.astype(jnp.bfloat16)
    rank = low.shape[1]
    local_slot = jnp.take(adapter_slot_index, token_adapter_index[:, 0], axis=0).astype(jnp.bfloat16)
    padded = -(-(rank + 1) // LANES) * LANES
    slot_col = jnp.zeros((total,), jnp.bfloat16).at[:rows].set(local_slot)
    payload = jnp.concatenate(
        [low, slot_col[:, None], jnp.zeros((total, padded - rank - 1), jnp.bfloat16)], axis=1
    )
    sent = jnp.broadcast_to(payload[None], (slots_held,) + payload.shape)
    gathered = lax.all_to_all(sent, "tensor", 0, 0, tiled=False)
    slots = gathered[:, :rows, rank].reshape(total).astype(jnp.int32)
    hits = slots[None, :, None] == jnp.arange(slots_held, dtype=jnp.int32)[:, None, None]
    spread = jnp.where(hits, gathered[:, :, :rank], jnp.zeros((), jnp.bfloat16))

    delta = jnp.einsum("str,srh->th", spread, adapter_up_weight, preferred_element_type=jnp.float32)
    return (jax.nn.silu(gate) * (up + delta)).astype(jnp.bfloat16)


def solution(mesh):
    in_specs = (
        P(("groups", "tensor"), None),
        P(None, "tensor"),
        P(None, "tensor"),
        P("tensor", None, None),
        P(None, None, "tensor"),
        P(("groups", "tensor"), None),
        P(),
    )
    out_specs = P("groups", "tensor")
    return jax.shard_map(body, mesh=mesh, in_specs=in_specs, out_specs=out_specs, check_vma=False)
```

```python
import jax
import jax.numpy as jnp
from jax import lax
from jax.experimental import pallas as pl
from jax.experimental.pallas import tpu as pltpu
from jax.sharding import PartitionSpec as P

SUBLANES = 8
BLOCK_ROWS = 1024


def _projection_kernel(order_ref, mine_ref, other_ref, gate_w_ref, up_w_ref, gate_ref, up_ref):
    k = pl.program_id(0)
    blocks = pl.num_programs(0) // 2

    @pl.when(k == 0)
    def _():
        gate_ref[...] = jnp.zeros_like(gate_ref)
        up_ref[...] = jnp.zeros_like(up_ref)

    def accumulate(x_ref):
        x = x_ref[...]
        gate_ref[...] += jnp.dot(x, gate_w_ref[...], preferred_element_type=jnp.float32)
        up_ref[...] += jnp.dot(x, up_w_ref[...], preferred_element_type=jnp.float32)

    pl.when(k < blocks)(lambda: accumulate(mine_ref))
    pl.when(k >= blocks)(lambda: accumulate(other_ref))


def projections(order, mine, other, gate_weight, up_weight):
    total, half = mine.shape
    hidden = gate_weight.shape[1]
    step = min(BLOCK_ROWS, half)
    blocks = half // step

    def weight_block(k, order_ref):
        first = order_ref[0] * blocks
        second = (1 - order_ref[0]) * blocks
        return (jnp.where(k < blocks, first + k, second + k - blocks), 0)

    weight_bytes = 2 * 2 * half * hidden * gate_weight.dtype.itemsize
    return pl.pallas_call(
        _projection_kernel,
        grid_spec=pltpu.PrefetchScalarGridSpec(
            num_scalar_prefetch=1,
            grid=(2 * blocks,),
            in_specs=[
                pl.BlockSpec((total, step), lambda k, o: (0, jnp.minimum(k, blocks - 1))),
                pl.BlockSpec((total, step), lambda k, o: (0, jnp.maximum(k - blocks, 0))),
                pl.BlockSpec((step, hidden), weight_block),
                pl.BlockSpec((step, hidden), weight_block),
            ],
            out_specs=[
                pl.BlockSpec((total, hidden), lambda k, o: (0, 0)),
                pl.BlockSpec((total, hidden), lambda k, o: (0, 0)),
            ],
        ),
        out_shape=[jax.ShapeDtypeStruct((total, hidden), jnp.float32)] * 2,
        compiler_params=pltpu.CompilerParams(dimension_semantics=("arbitrary",)),
        cost_estimate=pl.CostEstimate(
            flops=4 * total * 2 * half * hidden,
            transcendentals=0,
            bytes_accessed=weight_bytes + total * 2 * half * 2 + 2 * total * hidden * 4,
        ),
    )(order, mine, other, gate_weight, up_weight)


def body(
    tokens,
    gate_weight,
    up_weight,
    adapter_down_weight,
    adapter_up_weight,
    token_adapter_index,
    adapter_slot_index,
):
    rows, width = tokens.shape
    slots_held = adapter_up_weight.shape[0]
    half = width // 2
    me = lax.axis_index("tensor")
    order = me % 2
    halves = jnp.stack([tokens[:, :half], tokens[:, half:]])
    copies = jnp.broadcast_to(halves[None], (slots_held // 2, 2, rows, half)).reshape(slots_held, rows, half)
    mine = lax.all_to_all(copies, "tensor", 0, 0, tiled=False).reshape(slots_held * rows, half)
    other = lax.ppermute(mine, "tensor", [(j, j ^ 1) for j in range(slots_held)])
    total = mine.shape[0]

    down = adapter_down_weight[0]
    low = jnp.dot(mine, lax.dynamic_slice_in_dim(down, order * half, half), preferred_element_type=jnp.float32)
    low = low + jnp.dot(other, lax.dynamic_slice_in_dim(down, (1 - order) * half, half), preferred_element_type=jnp.float32)
    low = low.astype(jnp.bfloat16)
    rank = low.shape[1]
    local_slot = jnp.take(adapter_slot_index, token_adapter_index[:, 0], axis=0).astype(jnp.bfloat16)
    slot_rows = jnp.zeros((SUBLANES, total), jnp.bfloat16).at[0, :rows].set(local_slot)
    payload = jnp.concatenate([low.T, slot_rows], axis=0)
    sent = jnp.broadcast_to(payload[None], (slots_held,) + payload.shape)
    gathered = lax.all_to_all(sent, "tensor", 0, 0, tiled=False)
    slots = gathered[:, rank, :rows].reshape(total).astype(jnp.int32)
    hits = slots[None, None, :] == jnp.arange(slots_held, dtype=jnp.int32)[:, None, None]
    spread = jnp.where(hits, gathered[:, :rank, :], jnp.zeros((), jnp.bfloat16))

    gate, up = projections(order.reshape(1).astype(jnp.int32), mine, other, gate_weight, up_weight)
    delta = jnp.einsum("srt,srh->th", spread, adapter_up_weight, preferred_element_type=jnp.float32)
    return (jax.nn.silu(gate) * (up + delta)).astype(jnp.bfloat16)


def solution(mesh):
    in_specs = (
        P(("groups", "tensor"), None),
        P(None, "tensor"),
        P(None, "tensor"),
        P("tensor", None, None),
        P(None, None, "tensor"),
        P(("groups", "tensor"), None),
        P(),
    )
    out_specs = P("groups", "tensor")
    return jax.shard_map(body, mesh=mesh, in_specs=in_specs, out_specs=out_specs, check_vma=False)
```

```python
import jax
import jax.numpy as jnp
from jax import lax
from jax.experimental import pallas as pl
from jax.experimental.pallas import tpu as pltpu
from jax.sharding import PartitionSpec as P

SUBLANES = 8
BLOCK_ROWS = 1024


def _projection_kernel(order_ref, mine_ref, other_ref, gate_w_ref, up_w_ref, gate_ref, up_ref):
    k = pl.program_id(0)
    blocks = pl.num_programs(0) // 2

    @pl.when(k == 0)
    def _():
        gate_ref[...] = jnp.zeros_like(gate_ref)
        up_ref[...] = jnp.zeros_like(up_ref)

    def accumulate(x_ref):
        x = x_ref[...]
        gate_ref[...] += jnp.dot(x, gate_w_ref[...], preferred_element_type=jnp.float32)
        up_ref[...] += jnp.dot(x, up_w_ref[...], preferred_element_type=jnp.float32)

    pl.when(k < blocks)(lambda: accumulate(mine_ref))
    pl.when(k >= blocks)(lambda: accumulate(other_ref))


def projections(order, mine, other, gate_weight, up_weight):
    total, half = mine.shape
    hidden = gate_weight.shape[1]
    step = min(BLOCK_ROWS, half)
    blocks = half // step

    def weight_block(k, order_ref):
        first = order_ref[0] * blocks
        second = (1 - order_ref[0]) * blocks
        return (jnp.where(k < blocks, first + k, second + k - blocks), 0)

    weight_bytes = 2 * 2 * half * hidden * gate_weight.dtype.itemsize
    return pl.pallas_call(
        _projection_kernel,
        grid_spec=pltpu.PrefetchScalarGridSpec(
            num_scalar_prefetch=1,
            grid=(2 * blocks,),
            in_specs=[
                pl.BlockSpec((total, step), lambda k, o: (0, jnp.minimum(k, blocks - 1))),
                pl.BlockSpec((total, step), lambda k, o: (0, jnp.maximum(k - blocks, 0))),
                pl.BlockSpec((step, hidden), weight_block),
                pl.BlockSpec((step, hidden), weight_block),
            ],
            out_specs=[
                pl.BlockSpec((total, hidden), lambda k, o: (0, 0)),
                pl.BlockSpec((total, hidden), lambda k, o: (0, 0)),
            ],
        ),
        out_shape=[jax.ShapeDtypeStruct((total, hidden), jnp.float32)] * 2,
        compiler_params=pltpu.CompilerParams(dimension_semantics=("arbitrary",)),
        cost_estimate=pl.CostEstimate(
            flops=4 * total * 2 * half * hidden,
            transcendentals=0,
            bytes_accessed=weight_bytes + total * 2 * half * 2 + 2 * total * hidden * 4,
        ),
    )(order, mine, other, gate_weight, up_weight)


def body(
    tokens,
    gate_weight,
    up_weight,
    adapter_down_weight,
    adapter_up_weight,
    token_adapter_index,
    adapter_slot_index,
):
    rows, width = tokens.shape
    slots_held = adapter_up_weight.shape[0]
    half = width // 2
    me = lax.axis_index("tensor")
    order = me % 2
    halves = jnp.stack([tokens[:, :half], tokens[:, half:]])
    copies = jnp.broadcast_to(halves[None], (slots_held // 2, 2, rows, half)).reshape(slots_held, rows, half)
    mine = lax.all_to_all(copies, "tensor", 0, 0, tiled=False).reshape(slots_held * rows, half)
    other = lax.ppermute(mine, "tensor", [(j, j ^ 1) for j in range(slots_held)])
    total = mine.shape[0]

    down = adapter_down_weight[0]
    low = jnp.dot(mine, lax.dynamic_slice_in_dim(down, order * half, half), preferred_element_type=jnp.float32)
    low = low + jnp.dot(other, lax.dynamic_slice_in_dim(down, (1 - order) * half, half), preferred_element_type=jnp.float32)
    low = low.astype(jnp.bfloat16)
    rank = low.shape[1]
    named = token_adapter_index[:, :1] == jnp.arange(adapter_slot_index.shape[0], dtype=jnp.int32)[None, :]
    local_slot = jnp.sum(jnp.where(named, adapter_slot_index[None, :], 0), axis=1).astype(jnp.bfloat16)
    slot_rows = jnp.zeros((SUBLANES, total), jnp.bfloat16).at[0, :rows].set(local_slot)
    payload = jnp.concatenate([low.T, slot_rows], axis=0)
    sent = jnp.broadcast_to(payload[None], (slots_held,) + payload.shape)
    gathered = lax.all_to_all(sent, "tensor", 0, 0, tiled=False)
    slots = gathered[:, rank, :rows].reshape(total).astype(jnp.int32)
    hits = slots[None, None, :] == jnp.arange(slots_held, dtype=jnp.int32)[:, None, None]
    spread = jnp.where(hits, gathered[:, :rank, :], jnp.zeros((), jnp.bfloat16))

    gate, up = projections(order.reshape(1).astype(jnp.int32), mine, other, gate_weight, up_weight)
    delta = jnp.einsum("srt,srh->th", spread, adapter_up_weight, preferred_element_type=jnp.float32)
    return (jax.nn.silu(gate) * (up + delta)).astype(jnp.bfloat16)


def solution(mesh):
    in_specs = (
        P(("groups", "tensor"), None),
        P(None, "tensor"),
        P(None, "tensor"),
        P("tensor", None, None),
        P(None, None, "tensor"),
        P(("groups", "tensor"), None),
        P(),
    )
    out_specs = P("groups", "tensor")
    return jax.shard_map(body, mesh=mesh, in_specs=in_specs, out_specs=out_specs, check_vma=False)
```

```python
import jax
import jax.numpy as jnp
from jax import lax
from jax.experimental import pallas as pl
from jax.experimental.pallas import tpu as pltpu
from jax.sharding import PartitionSpec as P

SUBLANES = 8
PIECES = 4


def _projection_kernel(block_ref, mine_ref, other_ref, gate_w_ref, up_w_ref, gate_ref, up_ref):
    k = pl.program_id(0)
    pieces = pl.num_programs(0) // 2

    @pl.when(k == 0)
    def _():
        gate_ref[...] = jnp.zeros_like(gate_ref)
        up_ref[...] = jnp.zeros_like(up_ref)

    def accumulate(x_ref):
        x = x_ref[...]
        gate_ref[...] += jnp.dot(x, gate_w_ref[...], preferred_element_type=jnp.float32)
        up_ref[...] += jnp.dot(x, up_w_ref[...], preferred_element_type=jnp.float32)

    pl.when(k < pieces)(lambda: accumulate(mine_ref))
    pl.when(k >= pieces)(lambda: accumulate(other_ref))


def projections(blocks, mine, other, gate_weight, up_weight):
    pieces, total, step = mine.shape
    width, hidden = gate_weight.shape
    weight_bytes = 2 * width * hidden * gate_weight.dtype.itemsize

    def weight_block(k, block_ref):
        return (block_ref[k], 0)

    return pl.pallas_call(
        _projection_kernel,
        grid_spec=pltpu.PrefetchScalarGridSpec(
            num_scalar_prefetch=1,
            grid=(2 * pieces,),
            in_specs=[
                pl.BlockSpec((None, total, step), lambda k, b: (jnp.minimum(k, pieces - 1), 0, 0)),
                pl.BlockSpec((None, total, step), lambda k, b: (jnp.maximum(k - pieces, 0), 0, 0)),
                pl.BlockSpec((step, hidden), weight_block),
                pl.BlockSpec((step, hidden), weight_block),
            ],
            out_specs=[
                pl.BlockSpec((total, hidden), lambda k, b: (0, 0)),
                pl.BlockSpec((total, hidden), lambda k, b: (0, 0)),
            ],
        ),
        out_shape=[jax.ShapeDtypeStruct((total, hidden), jnp.float32)] * 2,
        compiler_params=pltpu.CompilerParams(dimension_semantics=("arbitrary",)),
        cost_estimate=pl.CostEstimate(
            flops=4 * total * width * hidden,
            transcendentals=0,
            bytes_accessed=weight_bytes + total * width * 2 + 2 * total * hidden * 4,
        ),
    )(blocks, mine, other, gate_weight, up_weight)


def body(
    tokens,
    gate_weight,
    up_weight,
    adapter_down_weight,
    adapter_up_weight,
    token_adapter_index,
    adapter_slot_index,
):
    rows, width = tokens.shape
    slots_held = adapter_up_weight.shape[0]
    half = width // 2
    piece = half // PIECES
    me = lax.axis_index("tensor")
    core = me % 2
    spot = (me // 2) % PIECES
    cuts = tokens.reshape(rows, 2, PIECES, piece).transpose(2, 1, 0, 3).reshape(1, 2 * PIECES, rows, piece)
    copies = jnp.broadcast_to(cuts, (slots_held // (2 * PIECES), 2 * PIECES, rows, piece))
    own = lax.all_to_all(copies.reshape(slots_held, rows, piece), "tensor", 0, 0, tiled=False)
    own = own.reshape(slots_held * rows, piece)
    masks = [2 * m for m in range(PIECES)]
    got = [own] + [lax.ppermute(own, "tensor", [(j, j ^ m) for j in range(slots_held)]) for m in masks[1:]]
    mine = jnp.stack(got)
    other = lax.ppermute(mine, "tensor", [(j, j ^ 1) for j in range(slots_held)])
    total = own.shape[0]
    spots = spot ^ jnp.arange(PIECES, dtype=jnp.int32)
    blocks = jnp.concatenate([core * PIECES + spots, (1 - core) * PIECES + spots]).astype(jnp.int32)

    down = adapter_down_weight[0].reshape(2 * PIECES, piece, -1)
    low = jnp.einsum("ktc,kcr->tr", mine, jnp.take(down, blocks[:PIECES], axis=0), preferred_element_type=jnp.float32)
    low = low + jnp.einsum("ktc,kcr->tr", other, jnp.take(down, blocks[PIECES:], axis=0), preferred_element_type=jnp.float32)
    low = low.astype(jnp.bfloat16)
    rank = low.shape[1]
    named = token_adapter_index[:, :1] == jnp.arange(adapter_slot_index.shape[0], dtype=jnp.int32)[None, :]
    local_slot = jnp.sum(jnp.where(named, adapter_slot_index[None, :], 0), axis=1).astype(jnp.bfloat16)
    slot_rows = jnp.zeros((SUBLANES, total), jnp.bfloat16).at[0, :rows].set(local_slot)
    payload = jnp.concatenate([low.T, slot_rows], axis=0)
    sent = jnp.broadcast_to(payload[None], (slots_held,) + payload.shape)
    gathered = lax.all_to_all(sent, "tensor", 0, 0, tiled=False)
    slots = gathered[:, rank, :rows].reshape(total).astype(jnp.int32)
    hits = slots[None, None, :] == jnp.arange(slots_held, dtype=jnp.int32)[:, None, None]
    spread = jnp.where(hits, gathered[:, :rank, :], jnp.zeros((), jnp.bfloat16))

    gate, up = projections(blocks, mine, other, gate_weight, up_weight)
    delta = jnp.einsum("srt,srh->th", spread, adapter_up_weight, preferred_element_type=jnp.float32)
    return (jax.nn.silu(gate) * (up + delta)).astype(jnp.bfloat16)


def solution(mesh):
    in_specs = (
        P(("groups", "tensor"), None),
        P(None, "tensor"),
        P(None, "tensor"),
        P("tensor", None, None),
        P(None, None, "tensor"),
        P(("groups", "tensor"), None),
        P(),
    )
    out_specs = P("groups", "tensor")
    return jax.shard_map(body, mesh=mesh, in_specs=in_specs, out_specs=out_specs, check_vma=False)
```

```python
import jax
import jax.numpy as jnp
from jax import lax
from jax.experimental import pallas as pl
from jax.experimental.pallas import tpu as pltpu
from jax.sharding import PartitionSpec as P

SUBLANES = 8
PIECES = 2


def _projection_kernel(block_ref, mine_ref, other_ref, gate_w_ref, up_w_ref, gate_ref, up_ref):
    k = pl.program_id(0)
    pieces = pl.num_programs(0) // 2

    @pl.when(k == 0)
    def _():
        gate_ref[...] = jnp.zeros_like(gate_ref)
        up_ref[...] = jnp.zeros_like(up_ref)

    def accumulate(x_ref):
        x = x_ref[...]
        gate_ref[...] += jnp.dot(x, gate_w_ref[...], preferred_element_type=jnp.float32)
        up_ref[...] += jnp.dot(x, up_w_ref[...], preferred_element_type=jnp.float32)

    pl.when(k < pieces)(lambda: accumulate(mine_ref))
    pl.when(k >= pieces)(lambda: accumulate(other_ref))


def projections(blocks, mine, other, gate_weight, up_weight):
    pieces, total, step = mine.shape
    width, hidden = gate_weight.shape
    weight_bytes = 2 * width * hidden * gate_weight.dtype.itemsize

    def weight_block(k, block_ref):
        return (block_ref[k], 0)

    return pl.pallas_call(
        _projection_kernel,
        grid_spec=pltpu.PrefetchScalarGridSpec(
            num_scalar_prefetch=1,
            grid=(2 * pieces,),
            in_specs=[
                pl.BlockSpec((None, total, step), lambda k, b: (jnp.minimum(k, pieces - 1), 0, 0)),
                pl.BlockSpec((None, total, step), lambda k, b: (jnp.maximum(k - pieces, 0), 0, 0)),
                pl.BlockSpec((step, hidden), weight_block),
                pl.BlockSpec((step, hidden), weight_block),
            ],
            out_specs=[
                pl.BlockSpec((total, hidden), lambda k, b: (0, 0)),
                pl.BlockSpec((total, hidden), lambda k, b: (0, 0)),
            ],
        ),
        out_shape=[jax.ShapeDtypeStruct((total, hidden), jnp.float32)] * 2,
        compiler_params=pltpu.CompilerParams(dimension_semantics=("arbitrary",)),
        cost_estimate=pl.CostEstimate(
            flops=4 * total * width * hidden,
            transcendentals=0,
            bytes_accessed=weight_bytes + total * width * 2 + 2 * total * hidden * 4,
        ),
    )(blocks, mine, other, gate_weight, up_weight)


def body(
    tokens,
    gate_weight,
    up_weight,
    adapter_down_weight,
    adapter_up_weight,
    token_adapter_index,
    adapter_slot_index,
):
    rows, width = tokens.shape
    slots_held = adapter_up_weight.shape[0]
    half = width // 2
    piece = half // PIECES
    me = lax.axis_index("tensor")
    core = me % 2
    spot = (me // 2) % PIECES
    cuts = tokens.reshape(rows, 2, PIECES, piece).transpose(2, 1, 0, 3).reshape(1, 2 * PIECES, rows, piece)
    copies = jnp.broadcast_to(cuts, (slots_held // (2 * PIECES), 2 * PIECES, rows, piece))
    own = lax.all_to_all(copies.reshape(slots_held, rows, piece), "tensor", 0, 0, tiled=False)
    own = own.reshape(slots_held * rows, piece)
    masks = [2 * m for m in range(PIECES)]
    got = [own] + [lax.ppermute(own, "tensor", [(j, j ^ m) for j in range(slots_held)]) for m in masks[1:]]
    mine = jnp.stack(got)
    other = lax.ppermute(mine, "tensor", [(j, j ^ 1) for j in range(slots_held)])
    total = own.shape[0]
    spots = spot ^ jnp.arange(PIECES, dtype=jnp.int32)
    blocks = jnp.concatenate([core * PIECES + spots, (1 - core) * PIECES + spots]).astype(jnp.int32)

    down = adapter_down_weight[0].reshape(2 * PIECES, piece, -1)
    low = jnp.einsum("ktc,kcr->tr", mine, jnp.take(down, blocks[:PIECES], axis=0), preferred_element_type=jnp.float32)
    low = low + jnp.einsum("ktc,kcr->tr", other, jnp.take(down, blocks[PIECES:], axis=0), preferred_element_type=jnp.float32)
    low = low.astype(jnp.bfloat16)
    rank = low.shape[1]
    named = token_adapter_index[:, :1] == jnp.arange(adapter_slot_index.shape[0], dtype=jnp.int32)[None, :]
    local_slot = jnp.sum(jnp.where(named, adapter_slot_index[None, :], 0), axis=1).astype(jnp.bfloat16)
    slot_rows = jnp.zeros((SUBLANES, total), jnp.bfloat16).at[0, :rows].set(local_slot)
    payload = jnp.concatenate([low.T, slot_rows], axis=0)
    sent = jnp.broadcast_to(payload[None], (slots_held,) + payload.shape)
    gathered = lax.all_to_all(sent, "tensor", 0, 0, tiled=False)
    slots = gathered[:, rank, :rows].reshape(total).astype(jnp.int32)
    hits = slots[None, None, :] == jnp.arange(slots_held, dtype=jnp.int32)[:, None, None]
    spread = jnp.where(hits, gathered[:, :rank, :], jnp.zeros((), jnp.bfloat16))

    gate, up = projections(blocks, mine, other, gate_weight, up_weight)
    delta = jnp.einsum("srt,srh->th", spread, adapter_up_weight, preferred_element_type=jnp.float32)
    return (jax.nn.silu(gate) * (up + delta)).astype(jnp.bfloat16)


def solution(mesh):
    in_specs = (
        P(("groups", "tensor"), None),
        P(None, "tensor"),
        P(None, "tensor"),
        P("tensor", None, None),
        P(None, None, "tensor"),
        P(("groups", "tensor"), None),
        P(),
    )
    out_specs = P("groups", "tensor")
    return jax.shard_map(body, mesh=mesh, in_specs=in_specs, out_specs=out_specs, check_vma=False)
```

```python
import jax
import jax.numpy as jnp
from jax import lax
from jax.experimental import pallas as pl
from jax.experimental.pallas import tpu as pltpu
from jax.sharding import PartitionSpec as P

SUBLANES = 8
BLOCK_ROWS = 1024


def _projection_kernel(order_ref, mine_ref, other_ref, gate_w_ref, up_w_ref, gate_ref, up_ref):
    k = pl.program_id(0)
    blocks = pl.num_programs(0) // 2

    @pl.when(k == 0)
    def _():
        gate_ref[...] = jnp.zeros_like(gate_ref)
        up_ref[...] = jnp.zeros_like(up_ref)

    def accumulate(x_ref):
        x = x_ref[...]
        gate_ref[...] += jnp.dot(x, gate_w_ref[...], preferred_element_type=jnp.float32)
        up_ref[...] += jnp.dot(x, up_w_ref[...], preferred_element_type=jnp.float32)

    pl.when(k < blocks)(lambda: accumulate(mine_ref))
    pl.when(k >= blocks)(lambda: accumulate(other_ref))


def projections(order, mine, other, gate_weight, up_weight):
    total, half = mine.shape
    hidden = gate_weight.shape[1]
    step = min(BLOCK_ROWS, half)
    blocks = half // step

    def weight_block(k, order_ref):
        first = order_ref[0] * blocks
        second = (1 - order_ref[0]) * blocks
        return (jnp.where(k < blocks, first + k, second + k - blocks), 0)

    weight_bytes = 2 * 2 * half * hidden * gate_weight.dtype.itemsize
    return pl.pallas_call(
        _projection_kernel,
        grid_spec=pltpu.PrefetchScalarGridSpec(
            num_scalar_prefetch=1,
            grid=(2 * blocks,),
            in_specs=[
                pl.BlockSpec((total, step), lambda k, o: (0, jnp.minimum(k, blocks - 1))),
                pl.BlockSpec((total, step), lambda k, o: (0, jnp.maximum(k - blocks, 0))),
                pl.BlockSpec((step, hidden), weight_block),
                pl.BlockSpec((step, hidden), weight_block),
            ],
            out_specs=[
                pl.BlockSpec((total, hidden), lambda k, o: (0, 0)),
                pl.BlockSpec((total, hidden), lambda k, o: (0, 0)),
            ],
        ),
        out_shape=[jax.ShapeDtypeStruct((total, hidden), jnp.float32)] * 2,
        compiler_params=pltpu.CompilerParams(dimension_semantics=("arbitrary",)),
        cost_estimate=pl.CostEstimate(
            flops=4 * total * 2 * half * hidden,
            transcendentals=0,
            bytes_accessed=weight_bytes + total * 2 * half * 2 + 2 * total * hidden * 4,
        ),
    )(order, mine, other, gate_weight, up_weight)


def body(
    tokens,
    gate_weight,
    up_weight,
    adapter_down_weight,
    adapter_up_weight,
    token_adapter_index,
    adapter_slot_index,
):
    rows, width = tokens.shape
    slots_held = adapter_up_weight.shape[0]
    half = width // 2
    me = lax.axis_index("tensor")
    order = me % 2
    halves = jnp.stack([tokens[:, :half], tokens[:, half:]])
    copies = jnp.broadcast_to(halves[None], (slots_held // 2, 2, rows, half)).reshape(slots_held, rows, half)
    mine = lax.all_to_all(copies, "tensor", 0, 0, tiled=False).reshape(slots_held * rows, half)
    other = lax.ppermute(mine, "tensor", [(j, j ^ 1) for j in range(slots_held)])
    total = mine.shape[0]

    partners = [(j, j ^ 1) for j in range(slots_held)]
    down = adapter_down_weight[0]
    lent = lax.ppermute(lax.dynamic_slice_in_dim(down, (1 - order) * half, half), "tensor", partners)
    low = jnp.dot(mine, lax.dynamic_slice_in_dim(down, order * half, half), preferred_element_type=jnp.float32)
    lent_part = jnp.dot(mine, lent, preferred_element_type=jnp.float32)
    low = (low + lax.ppermute(lent_part, "tensor", partners)).astype(jnp.bfloat16)
    rank = low.shape[1]
    local_slot = jnp.take(adapter_slot_index, token_adapter_index[:, 0], axis=0).astype(jnp.bfloat16)
    slot_rows = jnp.zeros((SUBLANES, total), jnp.bfloat16).at[0, :rows].set(local_slot)
    payload = jnp.concatenate([low.T, slot_rows], axis=0)
    sent = jnp.broadcast_to(payload[None], (slots_held,) + payload.shape)
    gathered = lax.all_to_all(sent, "tensor", 0, 0, tiled=False)
    slots = gathered[:, rank, :rows].reshape(total).astype(jnp.int32)
    hits = slots[None, None, :] == jnp.arange(slots_held, dtype=jnp.int32)[:, None, None]
    spread = jnp.where(hits, gathered[:, :rank, :], jnp.zeros((), jnp.bfloat16))

    gate, up = projections(order.reshape(1).astype(jnp.int32), mine, other, gate_weight, up_weight)
    delta = jnp.einsum("srt,srh->th", spread, adapter_up_weight, preferred_element_type=jnp.float32)
    return (jax.nn.silu(gate) * (up + delta)).astype(jnp.bfloat16)


def solution(mesh):
    in_specs = (
        P(("groups", "tensor"), None),
        P(None, "tensor"),
        P(None, "tensor"),
        P("tensor", None, None),
        P(None, None, "tensor"),
        P(("groups", "tensor"), None),
        P(),
    )
    out_specs = P("groups", "tensor")
    return jax.shard_map(body, mesh=mesh, in_specs=in_specs, out_specs=out_specs, check_vma=False)
```

```python
import jax
import jax.numpy as jnp
from jax import lax
from jax.experimental import pallas as pl
from jax.experimental.pallas import tpu as pltpu
from jax.sharding import PartitionSpec as P

SUBLANES = 8
BLOCK_ROWS = 1024


def _projection_kernel(order_ref, mine_ref, other_ref, gate_w_ref, up_w_ref, gate_ref, up_ref):
    k = pl.program_id(0)
    blocks = pl.num_programs(0) // 2

    @pl.when(k == 0)
    def _():
        gate_ref[...] = jnp.zeros_like(gate_ref)
        up_ref[...] = jnp.zeros_like(up_ref)

    def accumulate(x_ref):
        x = x_ref[...]
        gate_ref[...] += jnp.dot(x, gate_w_ref[...], preferred_element_type=jnp.float32)
        up_ref[...] += jnp.dot(x, up_w_ref[...], preferred_element_type=jnp.float32)

    pl.when(k < blocks)(lambda: accumulate(mine_ref))
    pl.when(k >= blocks)(lambda: accumulate(other_ref))


def projections(order, mine, other, gate_weight, up_weight):
    total, half = mine.shape
    hidden = gate_weight.shape[1]
    step = min(BLOCK_ROWS, half)
    blocks = half // step

    def weight_block(k, order_ref):
        first = order_ref[0] * blocks
        second = (1 - order_ref[0]) * blocks
        return (jnp.where(k < blocks, first + k, second + k - blocks), 0)

    weight_bytes = 2 * 2 * half * hidden * gate_weight.dtype.itemsize
    return pl.pallas_call(
        _projection_kernel,
        grid_spec=pltpu.PrefetchScalarGridSpec(
            num_scalar_prefetch=1,
            grid=(2 * blocks,),
            in_specs=[
                pl.BlockSpec((total, step), lambda k, o: (0, jnp.minimum(k, blocks - 1))),
                pl.BlockSpec((total, step), lambda k, o: (0, jnp.maximum(k - blocks, 0))),
                pl.BlockSpec((step, hidden), weight_block),
                pl.BlockSpec((step, hidden), weight_block),
            ],
            out_specs=[
                pl.BlockSpec((total, hidden), lambda k, o: (0, 0)),
                pl.BlockSpec((total, hidden), lambda k, o: (0, 0)),
            ],
        ),
        out_shape=[jax.ShapeDtypeStruct((total, hidden), jnp.float32)] * 2,
        compiler_params=pltpu.CompilerParams(dimension_semantics=("arbitrary",)),
        cost_estimate=pl.CostEstimate(
            flops=4 * total * 2 * half * hidden,
            transcendentals=0,
            bytes_accessed=weight_bytes + total * 2 * half * 2 + 2 * total * hidden * 4,
        ),
    )(order, mine, other, gate_weight, up_weight)


def body(
    tokens,
    gate_weight,
    up_weight,
    adapter_down_weight,
    adapter_up_weight,
    token_adapter_index,
    adapter_slot_index,
):
    rows, width = tokens.shape
    slots_held = adapter_up_weight.shape[0]
    half = width // 2
    me = lax.axis_index("tensor")
    order = me % 2
    halves = jnp.stack([tokens[:, :half], tokens[:, half:]])
    copies = jnp.broadcast_to(halves[None], (slots_held // 2, 2, rows, half)).reshape(slots_held, rows, half)
    mine = lax.all_to_all(copies, "tensor", 0, 0, tiled=False).reshape(slots_held * rows, half)
    other = lax.ppermute(mine, "tensor", [(j, j ^ 1) for j in range(slots_held)])
    total = mine.shape[0]

    partners = [(j, j ^ 1) for j in range(slots_held)]
    down = adapter_down_weight[0]
    lent = lax.ppermute(lax.dynamic_slice_in_dim(down, (1 - order) * half, half), "tensor", partners)
    low = jnp.dot(mine, lax.dynamic_slice_in_dim(down, order * half, half), preferred_element_type=jnp.float32)
    lent_part = jnp.dot(mine, lent, preferred_element_type=jnp.float32)
    low = (low + lax.ppermute(lent_part, "tensor", partners)).astype(jnp.bfloat16)
    rank = low.shape[1]
    local_slot = jnp.take(adapter_slot_index, token_adapter_index[:, 0], axis=0).astype(jnp.bfloat16)
    slot_rows = jnp.zeros((SUBLANES, total), jnp.bfloat16).at[0, :rows].set(local_slot)
    payload = jnp.concatenate([low.T, slot_rows], axis=0)
    sent = jnp.broadcast_to(payload[None], (slots_held,) + payload.shape)
    gathered = lax.all_to_all(sent, "tensor", 0, 0, tiled=False)
    gate, up = projections(order.reshape(1).astype(jnp.int32), mine, other, gate_weight, up_weight)
    gathered, gate, up = lax.optimization_barrier((gathered, gate, up))
    slots = gathered[:, rank, :rows].reshape(total).astype(jnp.int32)
    hits = slots[None, None, :] == jnp.arange(slots_held, dtype=jnp.int32)[:, None, None]
    spread = jnp.where(hits, gathered[:, :rank, :], jnp.zeros((), jnp.bfloat16))

    delta = jnp.einsum("srt,srh->th", spread, adapter_up_weight, preferred_element_type=jnp.float32)
    return (jax.nn.silu(gate) * (up + delta)).astype(jnp.bfloat16)


def solution(mesh):
    in_specs = (
        P(("groups", "tensor"), None),
        P(None, "tensor"),
        P(None, "tensor"),
        P("tensor", None, None),
        P(None, None, "tensor"),
        P(("groups", "tensor"), None),
        P(),
    )
    out_specs = P("groups", "tensor")
    return jax.shard_map(body, mesh=mesh, in_specs=in_specs, out_specs=out_specs, check_vma=False)
```

```python
import jax
import jax.numpy as jnp
from jax import lax
from jax.experimental import pallas as pl
from jax.experimental.pallas import tpu as pltpu
from jax.sharding import PartitionSpec as P

SUBLANES = 8
BLOCK_ROWS = 1024


def _projection_kernel(order_ref, mine_ref, other_ref, gate_w_ref, up_w_ref, gate_ref, up_ref):
    k = pl.program_id(0)
    blocks = pl.num_programs(0) // 2

    @pl.when(k == 0)
    def _():
        gate_ref[...] = jnp.zeros_like(gate_ref)
        up_ref[...] = jnp.zeros_like(up_ref)

    def accumulate(x_ref):
        x = x_ref[...]
        gate_ref[...] += jnp.dot(x, gate_w_ref[...], preferred_element_type=jnp.float32)
        up_ref[...] += jnp.dot(x, up_w_ref[...], preferred_element_type=jnp.float32)

    pl.when(k < blocks)(lambda: accumulate(mine_ref))
    pl.when(k >= blocks)(lambda: accumulate(other_ref))

    @pl.when(k == 2 * blocks - 1)
    def _():
        gate_ref[...] = jax.nn.silu(gate_ref[...])


def projections(order, mine, other, gate_weight, up_weight):
    total, half = mine.shape
    hidden = gate_weight.shape[1]
    step = min(BLOCK_ROWS, half)
    blocks = half // step

    def weight_block(k, order_ref):
        first = order_ref[0] * blocks
        second = (1 - order_ref[0]) * blocks
        return (jnp.where(k < blocks, first + k, second + k - blocks), 0)

    weight_bytes = 2 * 2 * half * hidden * gate_weight.dtype.itemsize
    return pl.pallas_call(
        _projection_kernel,
        grid_spec=pltpu.PrefetchScalarGridSpec(
            num_scalar_prefetch=1,
            grid=(2 * blocks,),
            in_specs=[
                pl.BlockSpec((total, step), lambda k, o: (0, jnp.minimum(k, blocks - 1))),
                pl.BlockSpec((total, step), lambda k, o: (0, jnp.maximum(k - blocks, 0))),
                pl.BlockSpec((step, hidden), weight_block),
                pl.BlockSpec((step, hidden), weight_block),
            ],
            out_specs=[
                pl.BlockSpec((total, hidden), lambda k, o: (0, 0)),
                pl.BlockSpec((total, hidden), lambda k, o: (0, 0)),
            ],
        ),
        out_shape=[jax.ShapeDtypeStruct((total, hidden), jnp.float32)] * 2,
        compiler_params=pltpu.CompilerParams(dimension_semantics=("arbitrary",)),
        cost_estimate=pl.CostEstimate(
            flops=4 * total * 2 * half * hidden,
            transcendentals=total * hidden,
            bytes_accessed=weight_bytes + total * 2 * half * 2 + 2 * total * hidden * 4,
        ),
    )(order, mine, other, gate_weight, up_weight)


def body(
    tokens,
    gate_weight,
    up_weight,
    adapter_down_weight,
    adapter_up_weight,
    token_adapter_index,
    adapter_slot_index,
):
    rows, width = tokens.shape
    slots_held = adapter_up_weight.shape[0]
    half = width // 2
    me = lax.axis_index("tensor")
    order = me % 2
    halves = jnp.stack([tokens[:, :half], tokens[:, half:]])
    copies = jnp.broadcast_to(halves[None], (slots_held // 2, 2, rows, half)).reshape(slots_held, rows, half)
    mine = lax.all_to_all(copies, "tensor", 0, 0, tiled=False).reshape(slots_held * rows, half)
    other = lax.ppermute(mine, "tensor", [(j, j ^ 1) for j in range(slots_held)])
    total = mine.shape[0]

    down = adapter_down_weight[0]
    low = jnp.dot(mine, lax.dynamic_slice_in_dim(down, order * half, half), preferred_element_type=jnp.float32)
    low = low + jnp.dot(other, lax.dynamic_slice_in_dim(down, (1 - order) * half, half), preferred_element_type=jnp.float32)
    low = low.astype(jnp.bfloat16)
    rank = low.shape[1]
    local_slot = jnp.take(adapter_slot_index, token_adapter_index[:, 0], axis=0).astype(jnp.bfloat16)
    slot_rows = jnp.zeros((SUBLANES, total), jnp.bfloat16).at[0, :rows].set(local_slot)
    payload = jnp.concatenate([low.T, slot_rows], axis=0)
    sent = jnp.broadcast_to(payload[None], (slots_held,) + payload.shape)
    gathered = lax.all_to_all(sent, "tensor", 0, 0, tiled=False)
    slots = gathered[:, rank, :rows].reshape(total).astype(jnp.int32)
    hits = slots[None, None, :] == jnp.arange(slots_held, dtype=jnp.int32)[:, None, None]
    spread = jnp.where(hits, gathered[:, :rank, :], jnp.zeros((), jnp.bfloat16))

    gated, up = projections(order.reshape(1).astype(jnp.int32), mine, other, gate_weight, up_weight)
    delta = jnp.einsum("srt,srh->th", spread, adapter_up_weight, preferred_element_type=jnp.float32)
    return (gated * (up + delta)).astype(jnp.bfloat16)


def solution(mesh):
    in_specs = (
        P(("groups", "tensor"), None),
        P(None, "tensor"),
        P(None, "tensor"),
        P("tensor", None, None),
        P(None, None, "tensor"),
        P(("groups", "tensor"), None),
        P(),
    )
    out_specs = P("groups", "tensor")
    return jax.shard_map(body, mesh=mesh, in_specs=in_specs, out_specs=out_specs, check_vma=False)
```

```python
import jax
import jax.numpy as jnp
from jax import lax
from jax.experimental import pallas as pl
from jax.experimental.pallas import tpu as pltpu
from jax.sharding import PartitionSpec as P

SUBLANES = 8
BLOCK_ROWS = 2048


def _projection_kernel(order_ref, mine_ref, other_ref, gate_w_ref, up_w_ref, gate_ref, up_ref):
    k = pl.program_id(0)
    blocks = pl.num_programs(0) // 2

    @pl.when(k == 0)
    def _():
        gate_ref[...] = jnp.zeros_like(gate_ref)
        up_ref[...] = jnp.zeros_like(up_ref)

    def accumulate(x_ref):
        x = x_ref[...]
        gate_ref[...] += jnp.dot(x, gate_w_ref[...], preferred_element_type=jnp.float32)
        up_ref[...] += jnp.dot(x, up_w_ref[...], preferred_element_type=jnp.float32)

    pl.when(k < blocks)(lambda: accumulate(mine_ref))
    pl.when(k >= blocks)(lambda: accumulate(other_ref))


def projections(order, mine, other, gate_weight, up_weight):
    total, half = mine.shape
    hidden = gate_weight.shape[1]
    step = min(BLOCK_ROWS, half)
    blocks = half // step

    def weight_block(k, order_ref):
        first = order_ref[0] * blocks
        second = (1 - order_ref[0]) * blocks
        return (jnp.where(k < blocks, first + k, second + k - blocks), 0)

    weight_bytes = 2 * 2 * half * hidden * gate_weight.dtype.itemsize
    return pl.pallas_call(
        _projection_kernel,
        grid_spec=pltpu.PrefetchScalarGridSpec(
            num_scalar_prefetch=1,
            grid=(2 * blocks,),
            in_specs=[
                pl.BlockSpec((total, step), lambda k, o: (0, jnp.minimum(k, blocks - 1))),
                pl.BlockSpec((total, step), lambda k, o: (0, jnp.maximum(k - blocks, 0))),
                pl.BlockSpec((step, hidden), weight_block),
                pl.BlockSpec((step, hidden), weight_block),
            ],
            out_specs=[
                pl.BlockSpec((total, hidden), lambda k, o: (0, 0)),
                pl.BlockSpec((total, hidden), lambda k, o: (0, 0)),
            ],
        ),
        out_shape=[jax.ShapeDtypeStruct((total, hidden), jnp.float32)] * 2,
        compiler_params=pltpu.CompilerParams(dimension_semantics=("arbitrary",)),
        cost_estimate=pl.CostEstimate(
            flops=4 * total * 2 * half * hidden,
            transcendentals=0,
            bytes_accessed=weight_bytes + total * 2 * half * 2 + 2 * total * hidden * 4,
        ),
    )(order, mine, other, gate_weight, up_weight)


def body(
    tokens,
    gate_weight,
    up_weight,
    adapter_down_weight,
    adapter_up_weight,
    token_adapter_index,
    adapter_slot_index,
):
    rows, width = tokens.shape
    slots_held = adapter_up_weight.shape[0]
    half = width // 2
    me = lax.axis_index("tensor")
    order = me % 2
    halves = jnp.stack([tokens[:, :half], tokens[:, half:]])
    copies = jnp.broadcast_to(halves[None], (slots_held // 2, 2, rows, half)).reshape(slots_held, rows, half)
    mine = lax.all_to_all(copies, "tensor", 0, 0, tiled=False).reshape(slots_held * rows, half)
    other = lax.ppermute(mine, "tensor", [(j, j ^ 1) for j in range(slots_held)])
    total = mine.shape[0]

    down = adapter_down_weight[0]
    low = jnp.dot(mine, lax.dynamic_slice_in_dim(down, order * half, half), preferred_element_type=jnp.float32)
    low = low + jnp.dot(other, lax.dynamic_slice_in_dim(down, (1 - order) * half, half), preferred_element_type=jnp.float32)
    low = low.astype(jnp.bfloat16)
    rank = low.shape[1]
    local_slot = jnp.take(adapter_slot_index, token_adapter_index[:, 0], axis=0).astype(jnp.bfloat16)
    slot_rows = jnp.zeros((SUBLANES, total), jnp.bfloat16).at[0, :rows].set(local_slot)
    payload = jnp.concatenate([low.T, slot_rows], axis=0)
    sent = jnp.broadcast_to(payload[None], (slots_held,) + payload.shape)
    gathered = lax.all_to_all(sent, "tensor", 0, 0, tiled=False)
    slots = gathered[:, rank, :rows].reshape(total).astype(jnp.int32)
    hits = slots[None, None, :] == jnp.arange(slots_held, dtype=jnp.int32)[:, None, None]
    spread = jnp.where(hits, gathered[:, :rank, :], jnp.zeros((), jnp.bfloat16))

    gate, up = projections(order.reshape(1).astype(jnp.int32), mine, other, gate_weight, up_weight)
    delta = jnp.einsum("srt,srh->th", spread, adapter_up_weight, preferred_element_type=jnp.float32)
    return (jax.nn.silu(gate) * (up + delta)).astype(jnp.bfloat16)


def solution(mesh):
    in_specs = (
        P(("groups", "tensor"), None),
        P(None, "tensor"),
        P(None, "tensor"),
        P("tensor", None, None),
        P(None, None, "tensor"),
        P(("groups", "tensor"), None),
        P(),
    )
    out_specs = P("groups", "tensor")
    return jax.shard_map(body, mesh=mesh, in_specs=in_specs, out_specs=out_specs, check_vma=False)
```

```python
import jax
import jax.numpy as jnp
from jax import lax
from jax.experimental import pallas as pl
from jax.experimental.pallas import tpu as pltpu
from jax.sharding import PartitionSpec as P

SUBLANES = 8
BLOCK_ROWS = 1024


def _projection_kernel(order_ref, mine_ref, other_ref, gate_w_ref, up_w_ref, gate_ref, up_ref):
    k = pl.program_id(0)
    blocks = pl.num_programs(0) // 2

    def accumulate(x_ref):
        x = x_ref[...]
        gate_ref[...] += jnp.dot(x, gate_w_ref[...], preferred_element_type=jnp.float32)
        up_ref[...] += jnp.dot(x, up_w_ref[...], preferred_element_type=jnp.float32)

    @pl.when(k == 0)
    def _():
        x = mine_ref[...]
        gate_ref[...] = jnp.dot(x, gate_w_ref[...], preferred_element_type=jnp.float32)
        up_ref[...] = jnp.dot(x, up_w_ref[...], preferred_element_type=jnp.float32)

    pl.when((k > 0) & (k < blocks))(lambda: accumulate(mine_ref))
    pl.when(k >= blocks)(lambda: accumulate(other_ref))


def projections(order, mine, other, gate_weight, up_weight):
    total, half = mine.shape
    hidden = gate_weight.shape[1]
    step = min(BLOCK_ROWS, half)
    blocks = half // step

    def weight_block(k, order_ref):
        first = order_ref[0] * blocks
        second = (1 - order_ref[0]) * blocks
        return (jnp.where(k < blocks, first + k, second + k - blocks), 0)

    weight_bytes = 2 * 2 * half * hidden * gate_weight.dtype.itemsize
    return pl.pallas_call(
        _projection_kernel,
        grid_spec=pltpu.PrefetchScalarGridSpec(
            num_scalar_prefetch=1,
            grid=(2 * blocks,),
            in_specs=[
                pl.BlockSpec((total, step), lambda k, o: (0, jnp.minimum(k, blocks - 1))),
                pl.BlockSpec((total, step), lambda k, o: (0, jnp.maximum(k - blocks, 0))),
                pl.BlockSpec((step, hidden), weight_block),
                pl.BlockSpec((step, hidden), weight_block),
            ],
            out_specs=[
                pl.BlockSpec((total, hidden), lambda k, o: (0, 0)),
                pl.BlockSpec((total, hidden), lambda k, o: (0, 0)),
            ],
        ),
        out_shape=[jax.ShapeDtypeStruct((total, hidden), jnp.float32)] * 2,
        compiler_params=pltpu.CompilerParams(dimension_semantics=("arbitrary",)),
        cost_estimate=pl.CostEstimate(
            flops=4 * total * 2 * half * hidden,
            transcendentals=0,
            bytes_accessed=weight_bytes + total * 2 * half * 2 + 2 * total * hidden * 4,
        ),
    )(order, mine, other, gate_weight, up_weight)


def body(
    tokens,
    gate_weight,
    up_weight,
    adapter_down_weight,
    adapter_up_weight,
    token_adapter_index,
    adapter_slot_index,
):
    rows, width = tokens.shape
    slots_held = adapter_up_weight.shape[0]
    half = width // 2
    me = lax.axis_index("tensor")
    order = me % 2
    halves = jnp.stack([tokens[:, :half], tokens[:, half:]])
    copies = jnp.broadcast_to(halves[None], (slots_held // 2, 2, rows, half)).reshape(slots_held, rows, half)
    mine = lax.all_to_all(copies, "tensor", 0, 0, tiled=False).reshape(slots_held * rows, half)
    other = lax.ppermute(mine, "tensor", [(j, j ^ 1) for j in range(slots_held)])
    total = mine.shape[0]

    down = adapter_down_weight[0]
    low = jnp.dot(mine, lax.dynamic_slice_in_dim(down, order * half, half), preferred_element_type=jnp.float32)
    low = low + jnp.dot(other, lax.dynamic_slice_in_dim(down, (1 - order) * half, half), preferred_element_type=jnp.float32)
    low = low.astype(jnp.bfloat16)
    rank = low.shape[1]
    local_slot = jnp.take(adapter_slot_index, token_adapter_index[:, 0], axis=0).astype(jnp.bfloat16)
    slot_rows = jnp.zeros((SUBLANES, total), jnp.bfloat16).at[0, :rows].set(local_slot)
    payload = jnp.concatenate([low.T, slot_rows], axis=0)
    sent = jnp.broadcast_to(payload[None], (slots_held,) + payload.shape)
    gathered = lax.all_to_all(sent, "tensor", 0, 0, tiled=False)
    slots = gathered[:, rank, :rows].reshape(total).astype(jnp.int32)
    hits = slots[None, None, :] == jnp.arange(slots_held, dtype=jnp.int32)[:, None, None]
    spread = jnp.where(hits, gathered[:, :rank, :], jnp.zeros((), jnp.bfloat16))

    gate, up = projections(order.reshape(1).astype(jnp.int32), mine, other, gate_weight, up_weight)
    delta = jnp.einsum("srt,srh->th", spread, adapter_up_weight, preferred_element_type=jnp.float32)
    return (jax.nn.silu(gate) * (up + delta)).astype(jnp.bfloat16)


def solution(mesh):
    in_specs = (
        P(("groups", "tensor"), None),
        P(None, "tensor"),
        P(None, "tensor"),
        P("tensor", None, None),
        P(None, None, "tensor"),
        P(("groups", "tensor"), None),
        P(),
    )
    out_specs = P("groups", "tensor")
    return jax.shard_map(body, mesh=mesh, in_specs=in_specs, out_specs=out_specs, check_vma=False)
```
